32 devices in a mesh: grp: 2 (over y), frame: 4 (over x, core), coil: 4 (over z).
Axes of the slice: x: 2, y: 2, z: 4, core: 2. Of those that a mesh axis runs over, the one named last changes fastest.
Arguments:
- images: bfloat16 [8, 2, 384, 384], P(('grp', 'frame')), parts along dimension 0, may hold values from -6 to 6
- coil_maps: bfloat16 [8, 2, 384, 384], P(('grp', 'coil')), parts along dimension 0, may hold values from -3 to 3
- kspace_data: float32 [8, 4, 2, 6, 128], P(('grp', 'frame'), 'coil'), parts along dimension 0, may hold values from -6 to 6
- spoke_angle: int32 [8, 6], P(('grp', 'frame')), parts along dimension 0, may hold values from 0 to 15
- band_row: int32 [8, 6], P(('grp', 'frame')), parts along dimension 0, may hold values from 0 to 256
- band_col: int32 [8, 6], P(('grp', 'frame')), parts along dimension 0, may hold values from 0 to 256
- kernel_rows: bfloat16 [16, 128, 128], replicated, may hold values from -0.5 to 0.5
- kernel_cols: bfloat16 [16, 128, 128], replicated, may hold values from -0.5 to 0.5
Outputs:
- updated: float32 [8, 2, 384, 384], P(('grp', 'frame')), parts along dimension 0
The draws below stay inside these ranges and needn't reach their ends.
There are 2 independent parts, one for each index of `grp`. The reference program is written for one: setup_inputs(seed, part) draws one part's arguments, and reference() takes and returns one part's arrays. A program takes and returns all parts, laid end to end along the dimension named above; an argument that names none is the same for every part. Nothing has to cross between parts.
All inputs are finite; a program needn't handle non-finite values.
Results may differ from the reference program's by a relative error of at most 0.0014.
Values may be sent and summed in bfloat16 or wider, within the bound.
No kernel may reach another device: no remote copies, remote signals or barrier semaphores. Data moves between devices by JAX's collectives and lax.ppermute only.
A program may use at most 64 MiB of HBM per device.

```python
import math
import jax
import jax.numpy as jnp
from jax import lax

N = 384
TILE = 128
PATCH = 128
ANGLES = 16
TILES = 6
FRAMES = 4
COILS = 4


def plant(entries, rng, least, high):
    shape = entries.shape
    index_at = [jax.random.randint(jax.random.fold_in(rng, axis), (), 0, shape[axis]) for axis in range(len(shape))]
    entries = entries.at[tuple(index_at)].set(least)
    longest = shape.index(max(shape))
    index_at[longest] = (index_at[longest] + 1) % shape[longest]
    return entries.at[tuple(index_at)].set(high)


def levels(key, dims, shards, least, high):
    factor_of, own = 1.0, jax.random.fold_in(key, 6)
    for axis_at, parts in shards:
        heights = jnp.exp(jax.random.uniform(jax.random.fold_in(own, axis_at), (parts,), jnp.float32, least / len(shards), high / len(shards)))
        factor_of = factor_of * jnp.repeat(heights, dims[axis_at] // parts).reshape([-1 if axis == axis_at else 1 for axis in range(len(dims))])
    return factor_of


def gaussian(key, shape, width, bound, pieces=(), kind=jnp.bfloat16):
    array = width * jax.random.normal(key, shape, jnp.float32)
    if pieces:
        array = array * levels(key, shape, pieces, -0.22, 0.18)
    return jnp.clip(array, -bound, bound).astype(kind)


def setup_inputs(seed: int = 0, part: int = 0) -> dict:
    keys = jax.random.split(jax.random.key(seed), 9)
    part_keys = jax.random.split(jax.random.fold_in(keys[8], part), 9)
    images = gaussian(part_keys[0], (FRAMES, 2, N, N), 1.0, 6.0, ((0, 4),))
    coil_maps = gaussian(part_keys[1], (COILS, 2, N, N), 0.2, 3.0, ((0, 4),))
    kspace_data = gaussian(part_keys[2], (FRAMES, COILS, 2, TILES, TILE), 0.5, 6.0, ((0, 4), (1, 4)), jnp.float32)
    spoke_angle = plant(jax.random.randint(part_keys[3], (FRAMES, TILES), 0, ANGLES), jax.random.fold_in(part_keys[3], 1), 0, ANGLES - 1).astype(jnp.int32)
    band_row = plant(jax.random.randint(part_keys[4], (FRAMES, TILES), 0, N - PATCH + 1), jax.random.fold_in(part_keys[4], 1), 0, N - PATCH).astype(jnp.int32)
    band_col = plant(jax.random.randint(part_keys[5], (FRAMES, TILES), 0, N - PATCH + 1), jax.random.fold_in(part_keys[5], 1), 0, N - PATCH).astype(jnp.int32)
    kernel_rows = gaussian(keys[6], (ANGLES, PATCH, TILE), PATCH ** -0.5, 0.5)
    kernel_cols = gaussian(keys[7], (ANGLES, TILE, PATCH), PATCH ** -0.5, 0.5)
    return {"images": images, "coil_maps": coil_maps, "kspace_data": kspace_data, "spoke_angle": spoke_angle, "band_row": band_row, "band_col": band_col, "kernel_rows": kernel_rows, "kernel_cols": kernel_cols}


SMOOTHING = 0.05
STEP_SIZE = 1.0
TV_WEIGHT = 0.2

def transform_table(extent):
    indices = jnp.arange(extent, dtype=jnp.int32)
    phases = indices[:, None] * indices[None, :] % extent
    angle_values = 2.0 * math.pi / extent * phases.astype(jnp.float32)
    scaling = 1.0 / math.sqrt(extent)
    return jnp.stack([jnp.cos(angle_values) * scaling, jnp.sin(angle_values) * scaling]).astype(jnp.bfloat16)

def combine_parts(products, direction):
    real_part = products[0, 0] + direction * products[1, 1]
    imaginary = products[0, 1] - direction * products[1, 0]
    return jnp.stack([real_part, imaginary])

def left_apply(transform, planes, direction):
    products = jnp.einsum('aij,bjk->abik', transform.astype(jnp.float32), planes.astype(jnp.float32))
    return combine_parts(products, direction)

def right_apply(transform, planes, direction):
    products = jnp.einsum('bij,ajk->abik', planes.astype(jnp.float32), transform.astype(jnp.float32))
    return combine_parts(products, direction)

def coil_gradient(transform, frame_image, coil_map, measured, angle_ids, row_first, col_first, kernel_rows, kernel_cols):
    extent = frame_image.shape[-1]
    patch_side = kernel_cols.shape[-1]
    map_planes = coil_map.astype(jnp.float32)
    image_planes = frame_image.astype(jnp.float32)
    coil_image = jnp.stack([map_planes[0] * image_planes[0] - map_planes[1] * image_planes[1], map_planes[0] * image_planes[1] + map_planes[1] * image_planes[0]]).astype(jnp.bfloat16)
    half_done = left_apply(transform, coil_image, 1.0).astype(jnp.bfloat16)
    kspace = right_apply(transform, half_done, 1.0).astype(jnp.bfloat16)
    offsets = jnp.arange(patch_side, dtype=jnp.int32)
    row_index = (row_first.astype(jnp.int32)[:, None] + offsets)[:, :, None]
    col_index = (col_first.astype(jnp.int32)[:, None] + offsets)[:, None, :]
    patches = kspace[:, row_index, col_index]
    row_weights = kernel_rows[angle_ids].astype(jnp.float32)
    col_weights = kernel_cols[angle_ids].astype(jnp.float32)
    contracted = jnp.einsum('ptrq,tjq->ptrj', patches.astype(jnp.float32), col_weights)
    predicted = lax.optimization_barrier(jnp.sum(contracted * row_weights[None], axis=2))
    residual = predicted - measured
    spread = (row_weights[None] * residual[:, :, None, :]).astype(jnp.bfloat16)
    spread_back = jnp.einsum('ptrj,tjq->ptrq', spread.astype(jnp.float32), col_weights)
    gridded = jnp.zeros((2, extent, extent), jnp.float32).at[:, row_index, col_index].add(spread_back)
    gridded = gridded.astype(jnp.bfloat16)
    half_back = left_apply(transform, gridded, -1.0).astype(jnp.bfloat16)
    coil_back = right_apply(transform, half_back, -1.0)
    return jnp.stack([map_planes[0] * coil_back[0] + map_planes[1] * coil_back[1], map_planes[0] * coil_back[1] - map_planes[1] * coil_back[0]])

def reference(images, coil_maps, kspace_data, spoke_angle, band_row, band_col, kernel_rows, kernel_cols):
    transform = transform_table(N)

    def frame_gradient(frame_number):
        frame_image = images[frame_number]

        def add_coil(coil_number, running):
            return running + coil_gradient(transform, frame_image, coil_maps[coil_number], kspace_data[frame_number, coil_number], spoke_angle[frame_number], band_row[frame_number], band_col[frame_number], kernel_rows, kernel_cols)
        return lax.fori_loop(0, COILS, add_coil, jnp.zeros((2, N, N), jnp.float32))
    data_grad = lax.map(frame_gradient, jnp.arange(FRAMES, dtype=jnp.int32))
    widened = images.astype(jnp.float32)
    change = widened[1:] - widened[:-1]
    normed = change / jnp.sqrt(lax.optimization_barrier(jnp.sum(change * change, axis=1, keepdims=True)) + SMOOTHING)
    zero_frame = jnp.zeros_like(normed[:1])
    padded = jnp.concatenate([zero_frame, normed, zero_frame], axis=0)
    tv_grad = padded[:-1] - padded[1:]
    return widened - STEP_SIZE * (data_grad + TV_WEIGHT * tv_grad)
```

```python
import math

import jax
import jax.numpy as jnp
from jax import lax
from jax.sharding import PartitionSpec as P

SMOOTHING = 0.05
STEP_SIZE = 1.0
TV_WEIGHT = 0.2


def padded(cells, sides, width):
    for axis, dim in sides:
        count = lax.axis_size(axis)
        ends = count - 1
        head = lax.slice_in_dim(cells, 0, width, axis=dim)
        tail = lax.slice_in_dim(cells, cells.shape[dim] - width, cells.shape[dim], axis=dim)
        cells = jnp.concatenate(
            [
                lax.ppermute(tail, axis, [(i, (i + 1) % count) for i in range(ends)]),
                cells,
                lax.ppermute(head, axis, [((i + 1) % count, i) for i in range(ends)]),
            ],
            axis=dim,
        )
    return cells


def transform_table(extent):
    indices = jnp.arange(extent, dtype=jnp.int32)
    phases = indices[:, None] * indices[None, :] % extent
    angle_values = 2.0 * math.pi / extent * phases.astype(jnp.float32)
    scaling = 1.0 / math.sqrt(extent)
    return jnp.stack([jnp.cos(angle_values) * scaling, jnp.sin(angle_values) * scaling]).astype(
        jnp.bfloat16
    )


def combine_parts(products, direction):
    real_part = products[0, 0] + direction * products[1, 1]
    imaginary = products[0, 1] - direction * products[1, 0]
    return jnp.stack([real_part, imaginary])


def apply_update(own_rows, extended, data_grad, first_frame, frame_total):
    widened = extended.astype(jnp.float32)
    change = widened[1:] - widened[:-1]
    position = first_frame - 1 + jnp.arange(change.shape[0], dtype=jnp.int32)
    inside = ((position >= 0) & (position <= frame_total - 2)).astype(jnp.float32)
    normed = inside[:, None, None, None] * (
        change / jnp.sqrt(jnp.sum(change * change, axis=1, keepdims=True) + SMOOTHING)
    )
    tv_grad = normed[:-1] - normed[1:]
    return own_rows.astype(jnp.float32) - STEP_SIZE * (data_grad + TV_WEIGHT * tv_grad)


def exchange_rows(coil_map, rows, coil_count, coil_index):
    received = [None] * coil_count
    received[0] = lax.dynamic_slice_in_dim(coil_map, coil_index * rows, rows, axis=1)
    for shift in range(1, coil_count):
        target = (coil_index + shift) % coil_count
        block = lax.dynamic_slice_in_dim(coil_map, target * rows, rows, axis=1)
        received[shift] = lax.ppermute(
            block, "coil", [(i, (i + shift) % coil_count) for i in range(coil_count)]
        )
    return jnp.stack(received)


def forward_residual(transform, frame_image, coil_map, measured, row_first, col_first, row_w, col_w):
    patch_side = col_w.shape[-1]
    map_planes = coil_map.astype(jnp.float32)
    image_planes = frame_image.astype(jnp.float32)
    coil_image = jnp.stack(
        [
            map_planes[0] * image_planes[0] - map_planes[1] * image_planes[1],
            map_planes[0] * image_planes[1] + map_planes[1] * image_planes[0],
        ]
    ).astype(jnp.bfloat16)
    products = jnp.einsum("aij,bjk->abik", transform, coil_image, preferred_element_type=jnp.float32)
    half_done = combine_parts(products, 1.0).astype(jnp.bfloat16)
    products = jnp.einsum("bij,ajk->abik", half_done, transform, preferred_element_type=jnp.float32)
    kspace = combine_parts(products, 1.0).astype(jnp.bfloat16)
    tiles = row_first.shape[0]
    patches = jnp.stack(
        [
            lax.dynamic_slice(kspace, (0, row_first[g], col_first[g]), (2, patch_side, patch_side))
            for g in range(tiles)
        ],
        axis=1,
    )
    contracted = jnp.einsum("pgrq,gjq->pgrj", patches, col_w, preferred_element_type=jnp.float32)
    predicted = jnp.sum(contracted * row_w.astype(jnp.float32)[None], axis=2)
    return predicted - measured


def backward_rows(transform, residuals, map_rows, row_first, col_first, row_w, col_w, coil_index):
    coil_count, _, rows, extent = map_rows.shape
    patch_side = col_w.shape[-1]
    spread = (row_w.astype(jnp.float32)[None, None] * residuals[:, :, :, None, :]).astype(jnp.bfloat16)
    spread_back = jnp.einsum("cpgrj,gjq->cpgrq", spread, col_w, preferred_element_type=jnp.float32)
    grid = jnp.zeros((coil_count, 2, extent, extent), jnp.float32)
    for g in range(row_first.shape[0]):
        start = (0, 0, row_first[g], col_first[g])
        window = lax.dynamic_slice(grid, start, (coil_count, 2, patch_side, patch_side))
        grid = lax.dynamic_update_slice(grid, window + spread_back[:, :, g], start)
    grid = grid.astype(jnp.bfloat16)
    row_table = lax.dynamic_slice_in_dim(transform, coil_index * rows, rows, axis=1)
    products = jnp.einsum("aij,cbjk->abcik", row_table, grid, preferred_element_type=jnp.float32)
    half_back = combine_parts(products, -1.0).astype(jnp.bfloat16)
    products = jnp.einsum("bcij,ajk->abcik", half_back, transform, preferred_element_type=jnp.float32)
    coil_back = combine_parts(products, -1.0)
    maps = map_rows.astype(jnp.float32)
    real_part = jnp.sum(maps[:, 0] * coil_back[0] + maps[:, 1] * coil_back[1], axis=0)
    imaginary = jnp.sum(maps[:, 0] * coil_back[1] - maps[:, 1] * coil_back[0], axis=0)
    return jnp.stack([real_part, imaginary])


def local(
    images, coil_maps, kspace_data, spoke_angle, band_row, band_col, kernel_rows, kernel_cols
):
    frame_count = images.shape[0]
    extent = images.shape[-1]
    coil_count = lax.axis_size("coil")
    coil_index = lax.axis_index("coil")
    rows = extent // coil_count
    transform = transform_table(extent)
    map_rows = exchange_rows(coil_maps[0], rows, coil_count, coil_index)
    first_frame = lax.axis_index("frame") * frame_count
    frame_total = lax.axis_size("frame") * frame_count
    extended = padded(images, (("frame", 0),), 1)
    row_w = kernel_rows[spoke_angle[0]]
    col_w = kernel_cols[spoke_angle[0]]
    residual = forward_residual(
        transform, images[0], coil_maps[0], kspace_data[0, 0], band_row[0], band_col[0], row_w, col_w
    )
    residuals = lax.all_gather(residual, "coil")
    sources = (coil_index - jnp.arange(coil_count, dtype=jnp.int32)) % coil_count
    residuals = jnp.take(residuals, sources, axis=0)
    grad_rows = backward_rows(
        transform, residuals, map_rows, band_row[0], band_col[0], row_w, col_w, coil_index
    )
    data_grad = lax.all_gather(grad_rows.astype(jnp.bfloat16), "coil", axis=1, tiled=True)
    data_grad = data_grad.astype(jnp.float32)[None]
    return apply_update(images, extended, data_grad, first_frame, frame_total)


def solution(mesh):
    in_specs = (
        P(("grp", "frame"), None, None, None),
        P(("grp", "coil"), None, None, None),
        P(("grp", "frame"), "coil", None, None, None),
        P(("grp", "frame"), None),
        P(("grp", "frame"), None),
        P(("grp", "frame"), None),
        P(),
        P(),
    )
    out_specs = P(("grp", "frame"), None, None, None)
    return jax.shard_map(local, mesh=mesh, in_specs=in_specs, out_specs=out_specs, check_vma=False)
```

```python
import math

import jax
import jax.numpy as jnp
from jax import lax
from jax.sharding import PartitionSpec as P

SMOOTHING = 0.05
STEP_SIZE = 1.0
TV_WEIGHT = 0.2


def padded(cells, sides, width):
    for axis, dim in sides:
        count = lax.axis_size(axis)
        ends = count - 1
        head = lax.slice_in_dim(cells, 0, width, axis=dim)
        tail = lax.slice_in_dim(cells, cells.shape[dim] - width, cells.shape[dim], axis=dim)
        cells = jnp.concatenate(
            [
                lax.ppermute(tail, axis, [(i, (i + 1) % count) for i in range(ends)]),
                cells,
                lax.ppermute(head, axis, [((i + 1) % count, i) for i in range(ends)]),
            ],
            axis=dim,
        )
    return cells


def transform_table(extent):
    indices = jnp.arange(extent, dtype=jnp.int32)
    phases = indices[:, None] * indices[None, :] % extent
    angle_values = 2.0 * math.pi / extent * phases.astype(jnp.float32)
    scaling = 1.0 / math.sqrt(extent)
    return jnp.stack([jnp.cos(angle_values) * scaling, jnp.sin(angle_values) * scaling]).astype(
        jnp.bfloat16
    )


def combine_parts(products, direction):
    real_part = products[0, 0] + direction * products[1, 1]
    imaginary = products[0, 1] - direction * products[1, 0]
    return jnp.stack([real_part, imaginary])


def apply_update(own_rows, extended, data_grad, first_frame, frame_total):
    widened = extended.astype(jnp.float32)
    change = widened[1:] - widened[:-1]
    position = first_frame - 1 + jnp.arange(change.shape[0], dtype=jnp.int32)
    inside = ((position >= 0) & (position <= frame_total - 2)).astype(jnp.float32)
    normed = inside[:, None, None, None] * (
        change / jnp.sqrt(jnp.sum(change * change, axis=1, keepdims=True) + SMOOTHING)
    )
    tv_grad = normed[:-1] - normed[1:]
    return own_rows.astype(jnp.float32) - STEP_SIZE * (data_grad + TV_WEIGHT * tv_grad)


def rotated(block, coil_count, shift):
    return lax.ppermute(block, "coil", [(i, (i + shift) % coil_count) for i in range(coil_count)])


def exchange_rows(coil_map, rows, coil_count, coil_index):
    received = [lax.dynamic_slice_in_dim(coil_map, coil_index * rows, rows, axis=1)]
    for shift in range(1, coil_count):
        target = (coil_index + shift) % coil_count
        block = lax.dynamic_slice_in_dim(coil_map, target * rows, rows, axis=1)
        received.append(rotated(block, coil_count, shift))
    return jnp.stack(received)


def selector(first_index, extent, patch_side):
    positions = jnp.arange(extent, dtype=jnp.int32)
    offsets = jnp.arange(patch_side, dtype=jnp.int32)
    wanted = first_index[:, None, None] + offsets[None, None, :]
    return (positions[None, :, None] == wanted).astype(jnp.bfloat16)


def pick_kernels(kernels, angle_ids):
    choice = (angle_ids[:, None] == jnp.arange(kernels.shape[0], dtype=jnp.int32)[None, :])
    flat = kernels.reshape(kernels.shape[0], -1)
    picked = jnp.dot(choice.astype(kernels.dtype), flat, preferred_element_type=jnp.float32)
    return picked.astype(kernels.dtype).reshape((angle_ids.shape[0],) + kernels.shape[1:])


def forward_residual(transform, frame_image, coil_map, measured, row_select, col_select, row_w, col_w):
    map_planes = coil_map.astype(jnp.float32)
    image_planes = frame_image.astype(jnp.float32)
    coil_image = jnp.stack(
        [
            map_planes[0] * image_planes[0] - map_planes[1] * image_planes[1],
            map_planes[0] * image_planes[1] + map_planes[1] * image_planes[0],
        ]
    ).astype(jnp.bfloat16)
    products = jnp.einsum("aij,bjk->abik", transform, coil_image, preferred_element_type=jnp.float32)
    half_done = combine_parts(products, 1.0).astype(jnp.bfloat16)
    products = jnp.einsum("bij,ajk->abik", half_done, transform, preferred_element_type=jnp.float32)
    kspace = combine_parts(products, 1.0).astype(jnp.bfloat16)
    picked_rows = jnp.einsum(
        "gir,pik->pgrk", row_select, kspace, preferred_element_type=jnp.float32
    ).astype(jnp.bfloat16)
    patches = jnp.einsum(
        "pgrk,gkq->pgrq", picked_rows, col_select, preferred_element_type=jnp.float32
    ).astype(jnp.bfloat16)
    contracted = jnp.einsum("pgrq,gjq->pgrj", patches, col_w, preferred_element_type=jnp.float32)
    predicted = jnp.sum(contracted * row_w.astype(jnp.float32)[None], axis=2)
    return predicted - measured


def backward_rows(transform, residuals, map_rows, row_select, col_select, row_w, col_w, coil_index):
    rows = map_rows.shape[2]
    spread = (row_w.astype(jnp.float32)[None, None] * residuals[:, :, :, None, :]).astype(jnp.bfloat16)
    spread_back = jnp.einsum("cpgrj,gjq->cpgrq", spread, col_w, preferred_element_type=jnp.float32)
    placed = jnp.einsum(
        "cpgrq,gkq->cpgrk", spread_back.astype(jnp.bfloat16), col_select,
        preferred_element_type=jnp.float32,
    ).astype(jnp.bfloat16)
    row_table = lax.dynamic_slice_in_dim(transform, coil_index * rows, rows, axis=1)
    table_at = jnp.einsum(
        "aij,gjr->aigr", row_table, row_select, preferred_element_type=jnp.float32
    ).astype(jnp.bfloat16)
    products = jnp.einsum("aigr,cbgrk->abcik", table_at, placed, preferred_element_type=jnp.float32)
    half_back = combine_parts(products, -1.0).astype(jnp.bfloat16)
    products = jnp.einsum("bcij,ajk->abcik", half_back, transform, preferred_element_type=jnp.float32)
    coil_back = combine_parts(products, -1.0)
    maps = map_rows.astype(jnp.float32)
    real_part = jnp.sum(maps[:, 0] * coil_back[0] + maps[:, 1] * coil_back[1], axis=0)
    imaginary = jnp.sum(maps[:, 0] * coil_back[1] - maps[:, 1] * coil_back[0], axis=0)
    return jnp.stack([real_part, imaginary])


def local(
    images, coil_maps, kspace_data, spoke_angle, band_row, band_col, kernel_rows, kernel_cols
):
    frame_count = images.shape[0]
    extent = images.shape[-1]
    patch_side = kernel_cols.shape[-1]
    coil_count = lax.axis_size("coil")
    coil_index = lax.axis_index("coil")
    rows = extent // coil_count
    transform = transform_table(extent)
    map_rows = exchange_rows(coil_maps[0], rows, coil_count, coil_index)
    first_frame = lax.axis_index("frame") * frame_count
    frame_total = lax.axis_size("frame") * frame_count
    extended = padded(images, (("frame", 0),), 1)
    row_w = pick_kernels(kernel_rows, spoke_angle[0])
    col_w = pick_kernels(kernel_cols, spoke_angle[0])
    row_select = selector(band_row[0], extent, patch_side)
    col_select = selector(band_col[0], extent, patch_side)
    residual = forward_residual(
        transform, images[0], coil_maps[0], kspace_data[0, 0], row_select, col_select, row_w, col_w
    )
    residuals = jnp.stack(
        [residual] + [rotated(residual, coil_count, shift) for shift in range(1, coil_count)]
    )
    grad_rows = backward_rows(
        transform, residuals, map_rows, row_select, col_select, row_w, col_w, coil_index
    )
    data_grad = lax.all_gather(grad_rows.astype(jnp.bfloat16), "coil", axis=1, tiled=True)
    data_grad = data_grad.astype(jnp.float32)[None]
    return apply_update(images, extended, data_grad, first_frame, frame_total)


def solution(mesh):
    in_specs = (
        P(("grp", "frame"), None, None, None),
        P(("grp", "coil"), None, None, None),
        P(("grp", "frame"), "coil", None, None, None),
        P(("grp", "frame"), None),
        P(("grp", "frame"), None),
        P(("grp", "frame"), None),
        P(),
        P(),
    )
    out_specs = P(("grp", "frame"), None, None, None)
    return jax.shard_map(local, mesh=mesh, in_specs=in_specs, out_specs=out_specs, check_vma=False)
```

```python
import math

import jax
import ml_dtypes
import numpy as np
import jax.numpy as jnp
from jax import lax
from jax.sharding import PartitionSpec as P


SMOOTHING = 0.05
STEP_SIZE = 1.0
TV_WEIGHT = 0.2


def padded(cells, sides, width):
    for axis, dim in sides:
        count = lax.axis_size(axis)
        ends = count - 1
        head = lax.slice_in_dim(cells, 0, width, axis=dim)
        tail = lax.slice_in_dim(cells, cells.shape[dim] - width, cells.shape[dim], axis=dim)
        cells = jnp.concatenate(
            [
                lax.ppermute(tail, axis, [(i, (i + 1) % count) for i in range(ends)]),
                cells,
                lax.ppermute(head, axis, [((i + 1) % count, i) for i in range(ends)]),
            ],
            axis=dim,
        )
    return cells


def transform_table(extent):
    indices = np.arange(extent, dtype=np.int64)
    phases = (indices[:, None] * indices[None, :] % extent).astype(np.float32)
    angle_values = np.float32(2.0 * math.pi / extent) * phases
    scaling = np.float32(1.0 / math.sqrt(extent))
    table = np.stack([np.cos(angle_values) * scaling, np.sin(angle_values) * scaling])
    return jnp.asarray(table.astype(ml_dtypes.bfloat16))


def combine_parts(products, direction):
    real_part = products[0, 0] + direction * products[1, 1]
    imaginary = products[0, 1] - direction * products[1, 0]
    return jnp.stack([real_part, imaginary])


def rotated(block, coil_count, shift):
    return lax.ppermute(block, "coil", [(i, (i + shift) % coil_count) for i in range(coil_count)])


def exchange_rows(coil_map, rows, coil_count, coil_index):
    received = [lax.dynamic_slice_in_dim(coil_map, coil_index * rows, rows, axis=1)]
    for shift in range(1, coil_count):
        target = (coil_index + shift) % coil_count
        block = lax.dynamic_slice_in_dim(coil_map, target * rows, rows, axis=1)
        received.append(rotated(block, coil_count, shift))
    return jnp.stack(received)


def selector(first_index, extent, patch_side):
    positions = jnp.arange(extent, dtype=jnp.int32)
    offsets = jnp.arange(patch_side, dtype=jnp.int32)
    wanted = first_index[:, None, None] + offsets[None, None, :]
    return (positions[None, :, None] == wanted).astype(jnp.bfloat16)


def pick_kernels(kernels, angle_ids):
    choice = (angle_ids[:, None] == jnp.arange(kernels.shape[0], dtype=jnp.int32)[None, :])
    flat = kernels.reshape(kernels.shape[0], -1)
    picked = jnp.dot(choice.astype(kernels.dtype), flat, preferred_element_type=jnp.float32)
    return picked.astype(kernels.dtype).reshape((angle_ids.shape[0],) + kernels.shape[1:])


def forward_residual(transform, frame_image, coil_map, measured, row_placed, col_placed):
    map_planes = coil_map.astype(jnp.float32)
    image_planes = frame_image.astype(jnp.float32)
    coil_image = jnp.stack(
        [
            map_planes[0] * image_planes[0] - map_planes[1] * image_planes[1],
            map_planes[0] * image_planes[1] + map_planes[1] * image_planes[0],
        ]
    ).astype(jnp.bfloat16)
    products = jnp.einsum("aij,bjk->abik", transform, coil_image, preferred_element_type=jnp.float32)
    half_done = combine_parts(products, 1.0).astype(jnp.bfloat16)
    products = jnp.einsum("bij,ajk->abik", half_done, transform, preferred_element_type=jnp.float32)
    kspace = combine_parts(products, 1.0).astype(jnp.bfloat16)
    contracted = jnp.einsum("pik,gjk->pgij", kspace, col_placed, preferred_element_type=jnp.float32)
    predicted = jnp.sum(contracted * row_placed.astype(jnp.float32)[None], axis=2)
    return predicted - measured


def backward_rows(transform, residuals, map_rows, row_select, row_w, col_placed, coil_index):
    rows = map_rows.shape[2]
    spread = (row_w.astype(jnp.float32)[None, None] * residuals[:, :, :, None, :]).astype(jnp.bfloat16)
    placed = jnp.einsum(
        "cpgrj,gjk->cpgrk", spread, col_placed, preferred_element_type=jnp.float32
    ).astype(jnp.bfloat16)
    row_table = lax.dynamic_slice_in_dim(transform, coil_index * rows, rows, axis=1)
    table_at = jnp.einsum(
        "aij,gjr->aigr", row_table, row_select, preferred_element_type=jnp.float32
    ).astype(jnp.bfloat16)
    products = jnp.einsum("aigr,cbgrk->abcik", table_at, placed, preferred_element_type=jnp.float32)
    half_back = combine_parts(products, -1.0).astype(jnp.bfloat16)
    products = jnp.einsum("bcij,ajk->abcik", half_back, transform, preferred_element_type=jnp.float32)
    coil_back = combine_parts(products, -1.0)
    maps = map_rows.astype(jnp.float32)
    real_part = jnp.sum(maps[:, 0] * coil_back[0] + maps[:, 1] * coil_back[1], axis=0)
    imaginary = jnp.sum(maps[:, 0] * coil_back[1] - maps[:, 1] * coil_back[0], axis=0)
    return jnp.stack([real_part, imaginary])


def tv_term(extended, first_frame, frame_total):
    widened = extended.astype(jnp.float32)
    change = widened[1:] - widened[:-1]
    position = first_frame - 1 + jnp.arange(change.shape[0], dtype=jnp.int32)
    inside = ((position >= 0) & (position <= frame_total - 2)).astype(jnp.float32)
    normed = inside[:, None, None, None] * (
        change / jnp.sqrt(jnp.sum(change * change, axis=1, keepdims=True) + SMOOTHING)
    )
    return normed[:-1] - normed[1:]


def local(
    images, coil_maps, kspace_data, spoke_angle, band_row, band_col, kernel_rows, kernel_cols
):
    frame_count = images.shape[0]
    extent = images.shape[-1]
    patch_side = kernel_cols.shape[-1]
    coil_count = lax.axis_size("coil")
    coil_index = lax.axis_index("coil")
    rows = extent // coil_count
    transform = transform_table(extent)
    map_rows = exchange_rows(coil_maps[0], rows, coil_count, coil_index)
    first_frame = lax.axis_index("frame") * frame_count
    frame_total = lax.axis_size("frame") * frame_count
    extended = padded(images, (("frame", 0),), 1)
    row_w = pick_kernels(kernel_rows, spoke_angle[0])
    col_w = pick_kernels(kernel_cols, spoke_angle[0])
    row_select = selector(band_row[0], extent, patch_side)
    col_select = selector(band_col[0], extent, patch_side)
    exact = dict(preferred_element_type=jnp.float32)
    col_placed = jnp.einsum("gjq,gkq->gjk", col_w, col_select, **exact).astype(jnp.bfloat16)
    row_placed = jnp.einsum("grj,gir->gij", row_w, row_select, **exact).astype(jnp.bfloat16)
    residual = forward_residual(
        transform, images[0], coil_maps[0], kspace_data[0, 0], row_placed, col_placed
    )
    residuals = jnp.stack(
        [residual] + [rotated(residual, coil_count, shift) for shift in range(1, coil_count)]
    )
    grad_rows = backward_rows(
        transform, residuals, map_rows, row_select, row_w, col_placed, coil_index
    )
    tv_grad = tv_term(extended, first_frame, frame_total)
    tv_grad, grad_rows = lax.optimization_barrier((tv_grad, grad_rows.astype(jnp.bfloat16)))
    data_grad = lax.all_gather(grad_rows, "coil", axis=1, tiled=True).astype(jnp.float32)[None]
    return images.astype(jnp.float32) - STEP_SIZE * (data_grad + TV_WEIGHT * tv_grad)


def solution(mesh):
    in_specs = (
        P(("grp", "frame"), None, None, None),
        P(("grp", "coil"), None, None, None),
        P(("grp", "frame"), "coil", None, None, None),
        P(("grp", "frame"), None),
        P(("grp", "frame"), None),
        P(("grp", "frame"), None),
        P(),
        P(),
    )
    out_specs = P(("grp", "frame"), None, None, None)
    return jax.shard_map(local, mesh=mesh, in_specs=in_specs, out_specs=out_specs, check_vma=False)
```

```python
import math

import jax
import ml_dtypes
import numpy as np
import jax.numpy as jnp
from jax import lax
from jax.sharding import PartitionSpec as P


SMOOTHING = 0.05
STEP_SIZE = 1.0
TV_WEIGHT = 0.2


def padded(cells, sides, width):
    for axis, dim in sides:
        count = lax.axis_size(axis)
        ends = count - 1
        head = lax.slice_in_dim(cells, 0, width, axis=dim)
        tail = lax.slice_in_dim(cells, cells.shape[dim] - width, cells.shape[dim], axis=dim)
        cells = jnp.concatenate(
            [
                lax.ppermute(tail, axis, [(i, (i + 1) % count) for i in range(ends)]),
                cells,
                lax.ppermute(head, axis, [((i + 1) % count, i) for i in range(ends)]),
            ],
            axis=dim,
        )
    return cells


def transform_table(extent):
    indices = np.arange(extent, dtype=np.int64)
    phases = (indices[:, None] * indices[None, :] % extent).astype(np.float32)
    angle_values = np.float32(2.0 * math.pi / extent) * phases
    scaling = np.float32(1.0 / math.sqrt(extent))
    table = np.stack([np.cos(angle_values) * scaling, np.sin(angle_values) * scaling])
    return jnp.asarray(table.astype(ml_dtypes.bfloat16))


def combine_parts(products, direction):
    real_part = products[0, 0] + direction * products[1, 1]
    imaginary = products[0, 1] - direction * products[1, 0]
    return jnp.stack([real_part, imaginary])


def rotated(block, coil_count, shift):
    return lax.ppermute(block, "coil", [(i, (i + shift) % coil_count) for i in range(coil_count)])


def exchange_rows(coil_map, rows, coil_count, coil_index):
    received = [lax.dynamic_slice_in_dim(coil_map, coil_index * rows, rows, axis=1)]
    for shift in range(1, coil_count):
        target = (coil_index + shift) % coil_count
        block = lax.dynamic_slice_in_dim(coil_map, target * rows, rows, axis=1)
        received.append(rotated(block, coil_count, shift))
    return jnp.stack(received)


def selector(first_index, extent, patch_side):
    positions = jnp.arange(extent, dtype=jnp.int32)
    offsets = jnp.arange(patch_side, dtype=jnp.int32)
    wanted = first_index[:, None, None] + offsets[None, None, :]
    return (positions[None, :, None] == wanted).astype(jnp.bfloat16)


def pick_kernels(kernels, angle_ids):
    choice = (angle_ids[:, None] == jnp.arange(kernels.shape[0], dtype=jnp.int32)[None, :])
    flat = kernels.reshape(kernels.shape[0], -1)
    picked = jnp.dot(choice.astype(kernels.dtype), flat, preferred_element_type=jnp.float32)
    return picked.astype(kernels.dtype).reshape((angle_ids.shape[0],) + kernels.shape[1:])


def forward_residual(transform, frame_image, coil_map, measured, row_placed, col_placed):
    map_planes = coil_map.astype(jnp.float32)
    image_planes = frame_image.astype(jnp.float32)
    coil_image = jnp.stack(
        [
            map_planes[0] * image_planes[0] - map_planes[1] * image_planes[1],
            map_planes[0] * image_planes[1] + map_planes[1] * image_planes[0],
        ]
    ).astype(jnp.bfloat16)
    products = jnp.einsum(
        "bij,ajk->abik", coil_image, transform, preferred_element_type=jnp.float32
    )
    half_done = combine_parts(products, 1.0).astype(jnp.bfloat16)
    products = jnp.einsum("aij,bjk->abik", transform, half_done, preferred_element_type=jnp.float32)
    kspace = combine_parts(products, 1.0).astype(jnp.bfloat16)
    contracted = jnp.einsum("pik,gjk->pgij", kspace, col_placed, preferred_element_type=jnp.float32)
    predicted = jnp.sum(contracted * row_placed.astype(jnp.float32)[None], axis=2)
    return predicted - measured


def backward_rows(transform, residuals, map_rows, row_select, row_w, col_placed, coil_index):
    rows = map_rows.shape[2]
    spread = (row_w.astype(jnp.float32)[None, None] * residuals[:, :, :, None, :]).astype(jnp.bfloat16)
    placed = jnp.einsum(
        "cpgrj,gjk->cpgrk", spread, col_placed, preferred_element_type=jnp.float32
    ).astype(jnp.bfloat16)
    row_table = lax.dynamic_slice_in_dim(transform, coil_index * rows, rows, axis=1)
    table_at = jnp.einsum(
        "aij,gjr->aigr", row_table, row_select, preferred_element_type=jnp.float32
    ).astype(jnp.bfloat16)
    products = jnp.einsum("aigr,cbgrk->abcik", table_at, placed, preferred_element_type=jnp.float32)
    half_back = combine_parts(products, -1.0).astype(jnp.bfloat16)
    products = jnp.einsum("bcij,ajk->abcik", half_back, transform, preferred_element_type=jnp.float32)
    coil_back = combine_parts(products, -1.0)
    maps = map_rows.astype(jnp.float32)
    real_part = jnp.sum(maps[:, 0] * coil_back[0] + maps[:, 1] * coil_back[1], axis=0)
    imaginary = jnp.sum(maps[:, 0] * coil_back[1] - maps[:, 1] * coil_back[0], axis=0)
    return jnp.stack([real_part, imaginary])


def tv_term(extended, first_frame, frame_total):
    widened = extended.astype(jnp.float32)
    change = widened[1:] - widened[:-1]
    position = first_frame - 1 + jnp.arange(change.shape[0], dtype=jnp.int32)
    inside = ((position >= 0) & (position <= frame_total - 2)).astype(jnp.float32)
    normed = inside[:, None, None, None] * (
        change / jnp.sqrt(jnp.sum(change * change, axis=1, keepdims=True) + SMOOTHING)
    )
    return normed[:-1] - normed[1:]


def normed_change(later, earlier, valid):
    change = later.astype(jnp.float32) - earlier.astype(jnp.float32)
    scale = jnp.sqrt(change[0] * change[0] + change[1] * change[1] + SMOOTHING)
    return valid * (change / scale)


def tv_single(images, frame_index, frame_total):
    count = lax.axis_size("frame")
    image = images[0]
    earlier = lax.ppermute(image, "frame", [(i, i + 1) for i in range(count - 1)])
    later = lax.ppermute(image, "frame", [(i + 1, i) for i in range(count - 1)])
    has_earlier = (frame_index >= 1).astype(jnp.float32)
    has_later = (frame_index <= frame_total - 2).astype(jnp.float32)
    return (normed_change(image, earlier, has_earlier) - normed_change(later, image, has_later))[None]


def body(
    images, coil_maps, kspace_data, spoke_angle, band_row, band_col, kernel_rows, kernel_cols
):
    frame_count = images.shape[0]
    extent = images.shape[-1]
    patch_side = kernel_cols.shape[-1]
    coil_count = lax.axis_size("coil")
    coil_index = lax.axis_index("coil")
    rows = extent // coil_count
    transform = transform_table(extent)
    map_rows = exchange_rows(coil_maps[0], rows, coil_count, coil_index)
    first_frame = lax.axis_index("frame") * frame_count
    frame_total = lax.axis_size("frame") * frame_count
    if frame_count == 1:
        tv_grad = tv_single(images, first_frame, frame_total)
    else:
        tv_grad = tv_term(padded(images, (("frame", 0),), 1), first_frame, frame_total)
    row_w = pick_kernels(kernel_rows, spoke_angle[0])
    col_w = pick_kernels(kernel_cols, spoke_angle[0])
    row_select = selector(band_row[0], extent, patch_side)
    col_select = selector(band_col[0], extent, patch_side)
    exact = dict(preferred_element_type=jnp.float32)
    col_placed = jnp.einsum("gjq,gkq->gjk", col_w, col_select, **exact).astype(jnp.bfloat16)
    row_placed = jnp.einsum("grj,gir->gij", row_w, row_select, **exact).astype(jnp.bfloat16)
    residual = forward_residual(
        transform, images[0], coil_maps[0], kspace_data[0, 0], row_placed, col_placed
    )
    residuals = jnp.stack(
        [residual] + [rotated(residual, coil_count, shift) for shift in range(1, coil_count)]
    )
    grad_rows = backward_rows(
        transform, residuals, map_rows, row_select, row_w, col_placed, coil_index
    )
    tv_grad, grad_rows = lax.optimization_barrier((tv_grad, grad_rows.astype(jnp.bfloat16)))
    data_grad = lax.all_gather(grad_rows, "coil", axis=1, tiled=True).astype(jnp.float32)[None]
    return images.astype(jnp.float32) - STEP_SIZE * (data_grad + TV_WEIGHT * tv_grad)


def solution(mesh):
    in_specs = (
        P(("grp", "frame"), None, None, None),
        P(("grp", "coil"), None, None, None),
        P(("grp", "frame"), "coil", None, None, None),
        P(("grp", "frame"), None),
        P(("grp", "frame"), None),
        P(("grp", "frame"), None),
        P(),
        P(),
    )
    out_specs = P(("grp", "frame"), None, None, None)
    return jax.shard_map(body, mesh=mesh, in_specs=in_specs, out_specs=out_specs, check_vma=False)
```

```python
import math

import jax
import ml_dtypes
import numpy as np
import jax.numpy as jnp
from jax import lax
from jax.sharding import PartitionSpec as P


SMOOTHING = 0.05
STEP_SIZE = 1.0
TV_WEIGHT = 0.2


def padded(cells, sides, width):
    for axis, dim in sides:
        count = lax.axis_size(axis)
        ends = count - 1
        head = lax.slice_in_dim(cells, 0, width, axis=dim)
        tail = lax.slice_in_dim(cells, cells.shape[dim] - width, cells.shape[dim], axis=dim)
        cells = jnp.concatenate(
            [
                lax.ppermute(tail, axis, [(i, (i + 1) % count) for i in range(ends)]),
                cells,
                lax.ppermute(head, axis, [((i + 1) % count, i) for i in range(ends)]),
            ],
            axis=dim,
        )
    return cells


def transform_table(extent):
    indices = np.arange(extent, dtype=np.int64)
    phases = (indices[:, None] * indices[None, :] % extent).astype(np.float32)
    angle_values = np.float32(2.0 * math.pi / extent) * phases
    scaling = np.float32(1.0 / math.sqrt(extent))
    table = np.stack([np.cos(angle_values) * scaling, np.sin(angle_values) * scaling])
    return jnp.asarray(table.astype(ml_dtypes.bfloat16))


def combine_parts(products, direction):
    real_part = products[0, 0] + direction * products[1, 1]
    imaginary = products[0, 1] - direction * products[1, 0]
    return jnp.stack([real_part, imaginary])


def rotated(block, coil_count, shift):
    return lax.ppermute(block, "coil", [(i, (i + shift) % coil_count) for i in range(coil_count)])


def exchange_rows(coil_map, rows, coil_count, coil_index):
    received = [lax.dynamic_slice_in_dim(coil_map, coil_index * rows, rows, axis=1)]
    for shift in range(1, coil_count):
        target = (coil_index + shift) % coil_count
        block = lax.dynamic_slice_in_dim(coil_map, target * rows, rows, axis=1)
        received.append(rotated(block, coil_count, shift))
    return jnp.stack(received)


def selector(first_index, extent, patch_side):
    positions = jnp.arange(extent, dtype=jnp.int32)
    offsets = jnp.arange(patch_side, dtype=jnp.int32)
    wanted = first_index[:, None, None] + offsets[None, None, :]
    return (positions[None, :, None] == wanted).astype(jnp.bfloat16)


def pick_kernels(kernels, angle_ids):
    choice = (angle_ids[:, None] == jnp.arange(kernels.shape[0], dtype=jnp.int32)[None, :])
    flat = kernels.reshape(kernels.shape[0], -1)
    picked = jnp.dot(choice.astype(kernels.dtype), flat, preferred_element_type=jnp.float32)
    return picked.astype(kernels.dtype).reshape((angle_ids.shape[0],) + kernels.shape[1:])


def forward_residual(transform, frame_image, coil_map, measured, row_placed, col_placed):
    map_planes = coil_map.astype(jnp.float32)
    image_planes = frame_image.astype(jnp.float32)
    coil_image = jnp.stack(
        [
            map_planes[0] * image_planes[0] - map_planes[1] * image_planes[1],
            map_planes[0] * image_planes[1] + map_planes[1] * image_planes[0],
        ]
    ).astype(jnp.bfloat16)
    products = jnp.einsum(
        "bij,ajk->abik", coil_image, transform, preferred_element_type=jnp.float32
    )
    half_done = combine_parts(products, 1.0).astype(jnp.bfloat16)
    products = jnp.einsum("aij,bjk->abik", transform, half_done, preferred_element_type=jnp.float32)
    kspace = combine_parts(products, 1.0).astype(jnp.bfloat16)
    contracted = jnp.einsum("pik,gjk->pgij", kspace, col_placed, preferred_element_type=jnp.float32)
    predicted = jnp.sum(contracted * row_placed.astype(jnp.float32)[None], axis=2)
    return predicted - measured


def backward_rows(transform, residuals, map_rows, row_select, row_w, col_placed, coil_index):
    coil_count, _, rows, extent = map_rows.shape
    spread = (row_w.astype(jnp.float32)[None, None] * residuals[:, :, :, None, :]).astype(jnp.bfloat16)
    placed = jnp.einsum(
        "cpgrj,gjk->pgrck", spread, col_placed, preferred_element_type=jnp.float32
    ).astype(jnp.bfloat16)
    row_table = lax.dynamic_slice_in_dim(transform, coil_index * rows, rows, axis=1)
    cos_rows, sin_rows = row_table[0], row_table[1]
    block = jnp.stack(
        [jnp.stack([cos_rows, -sin_rows], axis=1), jnp.stack([sin_rows, cos_rows], axis=1)]
    )
    block_at = jnp.einsum(
        "oibj,gjr->oibgr", block, row_select, preferred_element_type=jnp.float32
    ).astype(jnp.bfloat16)
    tiles, patch_side = row_select.shape[0], row_select.shape[2]
    half_back = jnp.dot(
        block_at.reshape(2 * rows, 2 * tiles * patch_side),
        placed.reshape(2 * tiles * patch_side, coil_count * extent),
        preferred_element_type=jnp.float32,
    ).astype(jnp.bfloat16).reshape(2, rows, coil_count, extent)
    products = jnp.einsum("bicj,ajk->abick", half_back, transform, preferred_element_type=jnp.float32)
    coil_back = combine_parts(products, -1.0)
    maps = jnp.transpose(map_rows, (1, 2, 0, 3)).astype(jnp.float32)
    real_part = jnp.sum(maps[0] * coil_back[0] + maps[1] * coil_back[1], axis=1)
    imaginary = jnp.sum(maps[0] * coil_back[1] - maps[1] * coil_back[0], axis=1)
    return jnp.stack([real_part, imaginary])


def tv_term(extended, first_frame, frame_total):
    widened = extended.astype(jnp.float32)
    change = widened[1:] - widened[:-1]
    position = first_frame - 1 + jnp.arange(change.shape[0], dtype=jnp.int32)
    inside = ((position >= 0) & (position <= frame_total - 2)).astype(jnp.float32)
    normed = inside[:, None, None, None] * (
        change / jnp.sqrt(jnp.sum(change * change, axis=1, keepdims=True) + SMOOTHING)
    )
    return normed[:-1] - normed[1:]


def normed_change(later, earlier, valid):
    change = later.astype(jnp.float32) - earlier.astype(jnp.float32)
    scale = jnp.sqrt(change[0] * change[0] + change[1] * change[1] + SMOOTHING)
    return valid * (change / scale)


def tv_single(images, frame_index, frame_total):
    count = lax.axis_size("frame")
    image = images[0]
    earlier = lax.ppermute(image, "frame", [(i, i + 1) for i in range(count - 1)])
    later = lax.ppermute(image, "frame", [(i + 1, i) for i in range(count - 1)])
    has_earlier = (frame_index >= 1).astype(jnp.float32)
    has_later = (frame_index <= frame_total - 2).astype(jnp.float32)
    return (normed_change(image, earlier, has_earlier) - normed_change(later, image, has_later))[None]


def body(
    images, coil_maps, kspace_data, spoke_angle, band_row, band_col, kernel_rows, kernel_cols
):
    frame_count = images.shape[0]
    extent = images.shape[-1]
    patch_side = kernel_cols.shape[-1]
    coil_count = lax.axis_size("coil")
    coil_index = lax.axis_index("coil")
    rows = extent // coil_count
    transform = transform_table(extent)
    map_rows = exchange_rows(coil_maps[0], rows, coil_count, coil_index)
    first_frame = lax.axis_index("frame") * frame_count
    frame_total = lax.axis_size("frame") * frame_count
    if frame_count == 1:
        tv_grad = tv_single(images, first_frame, frame_total)
    else:
        tv_grad = tv_term(padded(images, (("frame", 0),), 1), first_frame, frame_total)
    row_w = pick_kernels(kernel_rows, spoke_angle[0])
    col_w = pick_kernels(kernel_cols, spoke_angle[0])
    row_select = selector(band_row[0], extent, patch_side)
    col_select = selector(band_col[0], extent, patch_side)
    exact = dict(preferred_element_type=jnp.float32)
    col_placed = jnp.einsum("gjq,gkq->gjk", col_w, col_select, **exact).astype(jnp.bfloat16)
    row_placed = jnp.einsum("grj,gir->gij", row_w, row_select, **exact).astype(jnp.bfloat16)
    residual = forward_residual(
        transform, images[0], coil_maps[0], kspace_data[0, 0], row_placed, col_placed
    )
    residuals = jnp.stack(
        [residual] + [rotated(residual, coil_count, shift) for shift in range(1, coil_count)]
    )
    grad_rows = backward_rows(
        transform, residuals, map_rows, row_select, row_w, col_placed, coil_index
    )
    tv_grad, grad_rows = lax.optimization_barrier((tv_grad, grad_rows.astype(jnp.bfloat16)))
    data_grad = lax.all_gather(grad_rows, "coil", axis=1, tiled=True).astype(jnp.float32)[None]
    return images.astype(jnp.float32) - STEP_SIZE * (data_grad + TV_WEIGHT * tv_grad)


def solution(mesh):
    in_specs = (
        P(("grp", "frame"), None, None, None),
        P(("grp", "coil"), None, None, None),
        P(("grp", "frame"), "coil", None, None, None),
        P(("grp", "frame"), None),
        P(("grp", "frame"), None),
        P(("grp", "frame"), None),
        P(),
        P(),
    )
    out_specs = P(("grp", "frame"), None, None, None)
    return jax.shard_map(body, mesh=mesh, in_specs=in_specs, out_specs=out_specs, check_vma=False)
```

```python
import math

import jax
import ml_dtypes
import numpy as np
import jax.numpy as jnp
from jax import lax
from jax.sharding import PartitionSpec as P


SMOOTHING = 0.05
STEP_SIZE = 1.0
TV_WEIGHT = 0.2


def padded(cells, sides, width):
    for axis, dim in sides:
        count = lax.axis_size(axis)
        ends = count - 1
        head = lax.slice_in_dim(cells, 0, width, axis=dim)
        tail = lax.slice_in_dim(cells, cells.shape[dim] - width, cells.shape[dim], axis=dim)
        cells = jnp.concatenate(
            [
                lax.ppermute(tail, axis, [(i, (i + 1) % count) for i in range(ends)]),
                cells,
                lax.ppermute(head, axis, [((i + 1) % count, i) for i in range(ends)]),
            ],
            axis=dim,
        )
    return cells


def transform_table(extent):
    indices = np.arange(extent, dtype=np.int64)
    phases = (indices[:, None] * indices[None, :] % extent).astype(np.float32)
    angle_values = np.float32(2.0 * math.pi / extent) * phases
    scaling = np.float32(1.0 / math.sqrt(extent))
    table = np.stack([np.cos(angle_values) * scaling, np.sin(angle_values) * scaling])
    return jnp.asarray(table.astype(ml_dtypes.bfloat16))


def combine_parts(products, direction):
    real_part = products[0, 0] + direction * products[1, 1]
    imaginary = products[0, 1] - direction * products[1, 0]
    return jnp.stack([real_part, imaginary])


def rotated(block, coil_count, shift):
    return lax.ppermute(block, "coil", [(i, (i + shift) % coil_count) for i in range(coil_count)])


def exchange_rows(coil_map, rows, coil_count, coil_index):
    received = [lax.dynamic_slice_in_dim(coil_map, coil_index * rows, rows, axis=1)]
    for shift in range(1, coil_count):
        target = (coil_index + shift) % coil_count
        block = lax.dynamic_slice_in_dim(coil_map, target * rows, rows, axis=1)
        received.append(rotated(block, coil_count, shift))
    return jnp.stack(received)


def selector(first_index, extent, patch_side):
    positions = jnp.arange(extent, dtype=jnp.int32)
    offsets = jnp.arange(patch_side, dtype=jnp.int32)
    wanted = first_index[:, None, None] + offsets[None, None, :]
    return (positions[None, :, None] == wanted).astype(jnp.bfloat16)


def pick_kernels(kernels, angle_ids):
    choice = (angle_ids[:, None] == jnp.arange(kernels.shape[0], dtype=jnp.int32)[None, :])
    flat = kernels.reshape(kernels.shape[0], -1)
    picked = jnp.dot(choice.astype(kernels.dtype), flat, preferred_element_type=jnp.float32)
    return picked.astype(kernels.dtype).reshape((angle_ids.shape[0],) + kernels.shape[1:])


def forward_residual(transform, block, frame_image, coil_map, measured, row_placed, col_placed):
    map_planes = coil_map.astype(jnp.float32)
    image_planes = frame_image.astype(jnp.float32)
    coil_image = jnp.stack(
        [
            map_planes[0] * image_planes[0] - map_planes[1] * image_planes[1],
            map_planes[0] * image_planes[1] + map_planes[1] * image_planes[0],
        ]
    ).astype(jnp.bfloat16)
    products = jnp.einsum(
        "bij,ajk->abik", coil_image, transform, preferred_element_type=jnp.float32
    )
    half_done = combine_parts(products, 1.0).astype(jnp.bfloat16)
    extent = transform.shape[-1]
    kspace = jnp.dot(
        block, half_done.reshape(2 * extent, extent), preferred_element_type=jnp.float32
    ).astype(jnp.bfloat16).reshape(2, extent, extent)
    contracted = jnp.einsum("pik,gjk->pgij", kspace, col_placed, preferred_element_type=jnp.float32)
    predicted = jnp.sum(contracted * row_placed[None], axis=2)
    return predicted - measured


def backward_rows(transform, block_t, residuals, map_rows, row_select, row_w, col_placed, coil_index):
    rows = map_rows.shape[2]
    spread = (row_w.astype(jnp.float32)[None, None] * residuals[:, :, :, None, :]).astype(jnp.bfloat16)
    placed = jnp.einsum(
        "cpgrj,gjk->cpgrk", spread, col_placed, preferred_element_type=jnp.float32
    ).astype(jnp.bfloat16)
    row_table = lax.dynamic_slice_in_dim(transform, coil_index * rows, rows, axis=1)
    table_at = jnp.einsum(
        "aij,gjr->aigr", row_table, row_select, preferred_element_type=jnp.float32
    ).astype(jnp.bfloat16)
    products = jnp.einsum("aigr,cbgrk->abcik", table_at, placed, preferred_element_type=jnp.float32)
    half_back = combine_parts(products, -1.0).astype(jnp.bfloat16)
    coil_count, extent = half_back.shape[1], half_back.shape[-1]
    side_by_side = jnp.transpose(half_back, (1, 2, 0, 3)).reshape(coil_count * rows, 2 * extent)
    coil_back = jnp.dot(side_by_side, block_t.T, preferred_element_type=jnp.float32)
    coil_back = coil_back.reshape(coil_count, rows, 2, extent)
    maps = map_rows.astype(jnp.float32)
    real_part = jnp.sum(maps[:, 0] * coil_back[:, :, 0] + maps[:, 1] * coil_back[:, :, 1], axis=0)
    imaginary = jnp.sum(maps[:, 0] * coil_back[:, :, 1] - maps[:, 1] * coil_back[:, :, 0], axis=0)
    return jnp.stack([real_part, imaginary])


def tv_term(extended, first_frame, frame_total):
    widened = extended.astype(jnp.float32)
    change = widened[1:] - widened[:-1]
    position = first_frame - 1 + jnp.arange(change.shape[0], dtype=jnp.int32)
    inside = ((position >= 0) & (position <= frame_total - 2)).astype(jnp.float32)
    normed = inside[:, None, None, None] * (
        change / jnp.sqrt(jnp.sum(change * change, axis=1, keepdims=True) + SMOOTHING)
    )
    return normed[:-1] - normed[1:]


def normed_change(later, earlier, valid):
    change = later.astype(jnp.float32) - earlier.astype(jnp.float32)
    scale = jnp.sqrt(change[0] * change[0] + change[1] * change[1] + SMOOTHING)
    return valid * (change / scale)


def tv_single(images, frame_index, frame_total):
    count = lax.axis_size("frame")
    image = images[0]
    earlier = lax.ppermute(image, "frame", [(i, i + 1) for i in range(count - 1)])
    later = lax.ppermute(image, "frame", [(i + 1, i) for i in range(count - 1)])
    has_earlier = (frame_index >= 1).astype(jnp.float32)
    has_later = (frame_index <= frame_total - 2).astype(jnp.float32)
    return (normed_change(image, earlier, has_earlier) - normed_change(later, image, has_later))[None]


def body(
    images, coil_maps, kspace_data, spoke_angle, band_row, band_col, kernel_rows, kernel_cols
):
    frame_count = images.shape[0]
    extent = images.shape[-1]
    patch_side = kernel_cols.shape[-1]
    coil_count = lax.axis_size("coil")
    coil_index = lax.axis_index("coil")
    rows = extent // coil_count
    transform = transform_table(extent)
    map_rows = exchange_rows(coil_maps[0], rows, coil_count, coil_index)
    first_frame = lax.axis_index("frame") * frame_count
    frame_total = lax.axis_size("frame") * frame_count
    if frame_count == 1:
        tv_grad = tv_single(images, first_frame, frame_total)
    else:
        tv_grad = tv_term(padded(images, (("frame", 0),), 1), first_frame, frame_total)
    row_w = pick_kernels(kernel_rows, spoke_angle[0])
    col_w = pick_kernels(kernel_cols, spoke_angle[0])
    row_select = selector(band_row[0], extent, patch_side)
    col_select = selector(band_col[0], extent, patch_side)
    exact = dict(preferred_element_type=jnp.float32)
    col_placed = jnp.einsum("gjq,gkq->gjk", col_w, col_select, **exact).astype(jnp.bfloat16)
    row_placed = jnp.einsum("grj,gir->gij", row_w, row_select, **exact)
    cos_t, sin_t = lax.optimization_barrier(transform)
    block = jnp.concatenate(
        [jnp.concatenate([cos_t, sin_t], axis=1), jnp.concatenate([-sin_t, cos_t], axis=1)]
    )
    block_t = jnp.concatenate(
        [jnp.concatenate([cos_t, -sin_t], axis=1), jnp.concatenate([sin_t, cos_t], axis=1)]
    )
    residual = forward_residual(
        transform, block, images[0], coil_maps[0], kspace_data[0, 0], row_placed, col_placed
    )
    residuals = jnp.stack(
        [residual] + [rotated(residual, coil_count, shift) for shift in range(1, coil_count)]
    )
    grad_rows = backward_rows(
        transform, block_t, residuals, map_rows, row_select, row_w, col_placed, coil_index
    )
    tv_grad, grad_rows = lax.optimization_barrier((tv_grad, grad_rows.astype(jnp.bfloat16)))
    data_grad = lax.all_gather(grad_rows, "coil", axis=1, tiled=True).astype(jnp.float32)[None]
    return images.astype(jnp.float32) - STEP_SIZE * (data_grad + TV_WEIGHT * tv_grad)


def solution(mesh):
    in_specs = (
        P(("grp", "frame"), None, None, None),
        P(("grp", "coil"), None, None, None),
        P(("grp", "frame"), "coil", None, None, None),
        P(("grp", "frame"), None),
        P(("grp", "frame"), None),
        P(("grp", "frame"), None),
        P(),
        P(),
    )
    out_specs = P(("grp", "frame"), None, None, None)
    return jax.shard_map(body, mesh=mesh, in_specs=in_specs, out_specs=out_specs, check_vma=False)
```

```python
import math

import jax
import ml_dtypes
import numpy as np
import jax.numpy as jnp
from jax import lax
from jax.experimental import pallas as pl
from jax.sharding import PartitionSpec as P


SMOOTHING = 0.05
STEP_SIZE = 1.0
TV_WEIGHT = 0.2


def padded(cells, sides, width):
    for axis, dim in sides:
        count = lax.axis_size(axis)
        ends = count - 1
        head = lax.slice_in_dim(cells, 0, width, axis=dim)
        tail = lax.slice_in_dim(cells, cells.shape[dim] - width, cells.shape[dim], axis=dim)
        cells = jnp.concatenate(
            [
                lax.ppermute(tail, axis, [(i, (i + 1) % count) for i in range(ends)]),
                cells,
                lax.ppermute(head, axis, [((i + 1) % count, i) for i in range(ends)]),
            ],
            axis=dim,
        )
    return cells


def transform_table(extent):
    indices = np.arange(extent, dtype=np.int64)
    phases = (indices[:, None] * indices[None, :] % extent).astype(np.float32)
    angle_values = np.float32(2.0 * math.pi / extent) * phases
    scaling = np.float32(1.0 / math.sqrt(extent))
    table = np.stack([np.cos(angle_values) * scaling, np.sin(angle_values) * scaling])
    return jnp.asarray(table.astype(ml_dtypes.bfloat16))


def combine_parts(products, direction):
    real_part = products[0, 0] + direction * products[1, 1]
    imaginary = products[0, 1] - direction * products[1, 0]
    return jnp.stack([real_part, imaginary])


def rotated(block, coil_count, shift):
    return lax.ppermute(block, "coil", [(i, (i + shift) % coil_count) for i in range(coil_count)])


def exchange_rows(coil_map, rows, coil_count, coil_index):
    received = [lax.dynamic_slice_in_dim(coil_map, coil_index * rows, rows, axis=1)]
    for shift in range(1, coil_count):
        target = (coil_index + shift) % coil_count
        block = lax.dynamic_slice_in_dim(coil_map, target * rows, rows, axis=1)
        received.append(rotated(block, coil_count, shift))
    return jnp.stack(received)


def selector(first_index, extent, patch_side):
    positions = jnp.arange(extent, dtype=jnp.int32)
    offsets = jnp.arange(patch_side, dtype=jnp.int32)
    wanted = first_index[:, None, None] + offsets[None, None, :]
    return (positions[None, :, None] == wanted).astype(jnp.bfloat16)


def pick_kernels(kernels, angle_ids):
    choice = (angle_ids[:, None] == jnp.arange(kernels.shape[0], dtype=jnp.int32)[None, :])
    flat = kernels.reshape(kernels.shape[0], -1)
    picked = jnp.dot(choice.astype(kernels.dtype), flat, preferred_element_type=jnp.float32)
    return picked.astype(kernels.dtype).reshape((angle_ids.shape[0],) + kernels.shape[1:])


def forward_residual(transform, frame_image, coil_map, measured, row_placed, col_placed):
    map_planes = coil_map.astype(jnp.float32)
    image_planes = frame_image.astype(jnp.float32)
    coil_image = jnp.stack(
        [
            map_planes[0] * image_planes[0] - map_planes[1] * image_planes[1],
            map_planes[0] * image_planes[1] + map_planes[1] * image_planes[0],
        ]
    ).astype(jnp.bfloat16)
    products = jnp.einsum(
        "bij,ajk->abik", coil_image, transform, preferred_element_type=jnp.float32
    )
    half_done = combine_parts(products, 1.0).astype(jnp.bfloat16)
    cos_t, sin_t = lax.optimization_barrier(transform)
    block = jnp.concatenate(
        [jnp.concatenate([cos_t, sin_t], axis=1), jnp.concatenate([-sin_t, cos_t], axis=1)]
    )
    extent = transform.shape[-1]
    kspace = jnp.dot(
        block, half_done.reshape(2 * extent, extent), preferred_element_type=jnp.float32
    ).astype(jnp.bfloat16).reshape(2, extent, extent)
    contracted = jnp.einsum("pik,gjk->pgij", kspace, col_placed, preferred_element_type=jnp.float32)
    predicted = jnp.sum(contracted * row_placed[None], axis=2)
    return predicted - measured


def _product_kernel(lhs_ref, rhs_ref, out_ref):
    tiles, _, planes, patch_side, width = rhs_ref.shape
    rhs = rhs_ref[...].reshape(tiles * planes * patch_side, width)
    out_ref[0] = jnp.dot(lhs_ref[...], rhs, preferred_element_type=jnp.float32).astype(out_ref.dtype)


def per_coil_product(lhs, rhs):
    tiles, count, planes, patch_side, width = rhs.shape
    height, depth = lhs.shape
    return pl.pallas_call(
        _product_kernel,
        out_shape=jax.ShapeDtypeStruct((count, height, width), jnp.bfloat16),
        grid=(count,),
        in_specs=[
            pl.BlockSpec((height, depth), lambda c: (0, 0)),
            pl.BlockSpec((tiles, 1, planes, patch_side, width), lambda c: (0, c, 0, 0, 0)),
        ],
        out_specs=pl.BlockSpec((1, height, width), lambda c: (c, 0, 0)),
        cost_estimate=pl.CostEstimate(
            flops=2 * count * height * depth * width,
            transcendentals=0,
            bytes_accessed=2 * (height * depth + count * depth * width + count * height * width),
        ),
    )(lhs, rhs)


def backward_rows(transform, residuals, map_rows, row_select, row_w, col_placed, coil_index):
    rows = map_rows.shape[2]
    spread = (row_w.astype(jnp.float32)[None, None] * residuals[:, :, :, None, :]).astype(jnp.bfloat16)
    placed = jnp.einsum(
        "cpgrj,gjk->gcprk", spread, col_placed, preferred_element_type=jnp.float32
    ).astype(jnp.bfloat16)
    row_table = lax.dynamic_slice_in_dim(transform, coil_index * rows, rows, axis=1)
    cos_rows, sin_rows = row_table[0], row_table[1]
    block = jnp.stack(
        [jnp.stack([cos_rows, -sin_rows], axis=1), jnp.stack([sin_rows, cos_rows], axis=1)]
    )
    block_at = jnp.einsum(
        "oibj,gjr->oigbr", block, row_select, preferred_element_type=jnp.float32
    ).astype(jnp.bfloat16)
    tiles, coil_count, planes, patch_side, extent = placed.shape
    half_back = per_coil_product(
        block_at.reshape(2 * rows, tiles * planes * patch_side), placed
    ).reshape(coil_count, 2, rows, extent)
    products = jnp.einsum("cbij,ajk->abcik", half_back, transform, preferred_element_type=jnp.float32)
    coil_back = combine_parts(products, -1.0)
    maps = map_rows.astype(jnp.float32)
    real_part = jnp.sum(maps[:, 0] * coil_back[0] + maps[:, 1] * coil_back[1], axis=0)
    imaginary = jnp.sum(maps[:, 0] * coil_back[1] - maps[:, 1] * coil_back[0], axis=0)
    return jnp.stack([real_part, imaginary])


def tv_term(extended, first_frame, frame_total):
    widened = extended.astype(jnp.float32)
    change = widened[1:] - widened[:-1]
    position = first_frame - 1 + jnp.arange(change.shape[0], dtype=jnp.int32)
    inside = ((position >= 0) & (position <= frame_total - 2)).astype(jnp.float32)
    normed = inside[:, None, None, None] * (
        change / jnp.sqrt(jnp.sum(change * change, axis=1, keepdims=True) + SMOOTHING)
    )
    return normed[:-1] - normed[1:]


def normed_change(later, earlier, valid):
    change = later.astype(jnp.float32) - earlier.astype(jnp.float32)
    scale = jnp.sqrt(change[0] * change[0] + change[1] * change[1] + SMOOTHING)
    return valid * (change / scale)


def tv_single(images, frame_index, frame_total):
    count = lax.axis_size("frame")
    image = images[0]
    earlier = lax.ppermute(image, "frame", [(i, i + 1) for i in range(count - 1)])
    later = lax.ppermute(image, "frame", [(i + 1, i) for i in range(count - 1)])
    has_earlier = (frame_index >= 1).astype(jnp.float32)
    has_later = (frame_index <= frame_total - 2).astype(jnp.float32)
    return (normed_change(image, earlier, has_earlier) - normed_change(later, image, has_later))[None]


def body(
    images, coil_maps, kspace_data, spoke_angle, band_row, band_col, kernel_rows, kernel_cols
):
    frame_count = images.shape[0]
    extent = images.shape[-1]
    patch_side = kernel_cols.shape[-1]
    coil_count = lax.axis_size("coil")
    coil_index = lax.axis_index("coil")
    rows = extent // coil_count
    transform = transform_table(extent)
    map_rows = exchange_rows(coil_maps[0], rows, coil_count, coil_index)
    first_frame = lax.axis_index("frame") * frame_count
    frame_total = lax.axis_size("frame") * frame_count
    if frame_count == 1:
        tv_grad = tv_single(images, first_frame, frame_total)
    else:
        tv_grad = tv_term(padded(images, (("frame", 0),), 1), first_frame, frame_total)
    row_w = pick_kernels(kernel_rows, spoke_angle[0])
    col_w = pick_kernels(kernel_cols, spoke_angle[0])
    row_select = selector(band_row[0], extent, patch_side)
    col_select = selector(band_col[0], extent, patch_side)
    exact = dict(preferred_element_type=jnp.float32)
    col_placed = jnp.einsum("gjq,gkq->gjk", col_w, col_select, **exact).astype(jnp.bfloat16)
    row_placed = jnp.einsum("grj,gir->gij", row_w, row_select, **exact)
    residual = forward_residual(
        transform, images[0], coil_maps[0], kspace_data[0, 0], row_placed, col_placed
    )
    residuals = jnp.stack(
        [residual] + [rotated(residual, coil_count, shift) for shift in range(1, coil_count)]
    )
    grad_rows = backward_rows(
        transform, residuals, map_rows, row_select, row_w, col_placed, coil_index
    )
    tv_grad, grad_rows = lax.optimization_barrier((tv_grad, grad_rows.astype(jnp.bfloat16)))
    data_grad = lax.all_gather(grad_rows, "coil", axis=1, tiled=True).astype(jnp.float32)[None]
    return images.astype(jnp.float32) - STEP_SIZE * (data_grad + TV_WEIGHT * tv_grad)


def solution(mesh):
    in_specs = (
        P(("grp", "frame"), None, None, None),
        P(("grp", "coil"), None, None, None),
        P(("grp", "frame"), "coil", None, None, None),
        P(("grp", "frame"), None),
        P(("grp", "frame"), None),
        P(("grp", "frame"), None),
        P(),
        P(),
    )
    out_specs = P(("grp", "frame"), None, None, None)
    return jax.shard_map(body, mesh=mesh, in_specs=in_specs, out_specs=out_specs, check_vma=False)
```

```python
import math

import jax
import ml_dtypes
import numpy as np
import jax.numpy as jnp
from jax import lax
from jax.sharding import PartitionSpec as P


SMOOTHING = 0.05
STEP_SIZE = 1.0
TV_WEIGHT = 0.2


def padded(cells, sides, width):
    for axis, dim in sides:
        count = lax.axis_size(axis)
        ends = count - 1
        head = lax.slice_in_dim(cells, 0, width, axis=dim)
        tail = lax.slice_in_dim(cells, cells.shape[dim] - width, cells.shape[dim], axis=dim)
        cells = jnp.concatenate(
            [
                lax.ppermute(tail, axis, [(i, (i + 1) % count) for i in range(ends)]),
                cells,
                lax.ppermute(head, axis, [((i + 1) % count, i) for i in range(ends)]),
            ],
            axis=dim,
        )
    return cells


def transform_table(extent):
    indices = np.arange(extent, dtype=np.int64)
    phases = (indices[:, None] * indices[None, :] % extent).astype(np.float32)
    angle_values = np.float32(2.0 * math.pi / extent) * phases
    scaling = np.float32(1.0 / math.sqrt(extent))
    table = np.stack([np.cos(angle_values) * scaling, np.sin(angle_values) * scaling])
    return jnp.asarray(table.astype(ml_dtypes.bfloat16))


def combine_parts(products, direction):
    real_part = products[0, 0] + direction * products[1, 1]
    imaginary = products[0, 1] - direction * products[1, 0]
    return jnp.stack([real_part, imaginary])


def partner(index, coil_count, shift):
    if coil_count & (coil_count - 1) == 0:
        return index ^ shift
    return (index + shift) % coil_count


def rotated(block, coil_count, shift):
    pairs = [(i, partner(i, coil_count, shift)) for i in range(coil_count)]
    return lax.ppermute(block, "coil", pairs)


def exchange_rows(coil_map, rows, coil_count, coil_index):
    received = [lax.dynamic_slice_in_dim(coil_map, coil_index * rows, rows, axis=1)]
    for shift in range(1, coil_count):
        target = partner(coil_index, coil_count, shift)
        block = lax.dynamic_slice_in_dim(coil_map, target * rows, rows, axis=1)
        received.append(rotated(block, coil_count, shift))
    return jnp.stack(received)


def selector(first_index, extent, patch_side):
    positions = jnp.arange(extent, dtype=jnp.int32)
    offsets = jnp.arange(patch_side, dtype=jnp.int32)
    wanted = first_index[:, None, None] + offsets[None, None, :]
    return (positions[None, :, None] == wanted).astype(jnp.bfloat16)


def pick_kernels(kernels, angle_ids):
    choice = (angle_ids[:, None] == jnp.arange(kernels.shape[0], dtype=jnp.int32)[None, :])
    flat = kernels.reshape(kernels.shape[0], -1)
    picked = jnp.dot(choice.astype(kernels.dtype), flat, preferred_element_type=jnp.float32)
    return picked.astype(kernels.dtype).reshape((angle_ids.shape[0],) + kernels.shape[1:])


def forward_residual(transform, frame_image, coil_map, measured, row_placed, col_placed):
    map_planes = coil_map.astype(jnp.float32)
    image_planes = frame_image.astype(jnp.float32)
    coil_image = jnp.stack(
        [
            map_planes[0] * image_planes[0] - map_planes[1] * image_planes[1],
            map_planes[0] * image_planes[1] + map_planes[1] * image_planes[0],
        ]
    ).astype(jnp.bfloat16)
    products = jnp.einsum(
        "bij,ajk->abik", coil_image, transform, preferred_element_type=jnp.float32
    )
    half_done = combine_parts(products, 1.0).astype(jnp.bfloat16)
    cos_t, sin_t = lax.optimization_barrier(transform)
    block = jnp.concatenate(
        [jnp.concatenate([cos_t, sin_t], axis=1), jnp.concatenate([-sin_t, cos_t], axis=1)]
    )
    extent = transform.shape[-1]
    kspace = jnp.dot(
        block, half_done.reshape(2 * extent, extent), preferred_element_type=jnp.float32
    ).astype(jnp.bfloat16).reshape(2, extent, extent)
    contracted = jnp.einsum("pik,gjk->pgij", kspace, col_placed, preferred_element_type=jnp.float32)
    predicted = jnp.sum(contracted * row_placed[None], axis=2)
    return predicted - measured


def backward_rows(transform, residuals, map_rows, row_select, row_w, col_placed, coil_index):
    rows = map_rows.shape[2]
    spread = (row_w.astype(jnp.float32)[None, None] * residuals[:, :, :, None, :]).astype(jnp.bfloat16)
    placed = jnp.einsum(
        "cpgrj,gjk->cpgrk", spread, col_placed, preferred_element_type=jnp.float32
    ).astype(jnp.bfloat16)
    row_table = lax.dynamic_slice_in_dim(transform, coil_index * rows, rows, axis=1)
    table_at = jnp.einsum(
        "aij,gjr->aigr", row_table, row_select, preferred_element_type=jnp.float32
    ).astype(jnp.bfloat16)
    products = jnp.einsum("aigr,cbgrk->abcik", table_at, placed, preferred_element_type=jnp.float32)
    half_back = combine_parts(products, -1.0).astype(jnp.bfloat16)
    products = jnp.einsum("bcij,ajk->abcik", half_back, transform, preferred_element_type=jnp.float32)
    coil_back = combine_parts(products, -1.0)
    maps = map_rows.astype(jnp.float32)
    real_part = jnp.sum(maps[:, 0] * coil_back[0] + maps[:, 1] * coil_back[1], axis=0)
    imaginary = jnp.sum(maps[:, 0] * coil_back[1] - maps[:, 1] * coil_back[0], axis=0)
    return jnp.stack([real_part, imaginary])


def tv_term(extended, first_frame, frame_total):
    widened = extended.astype(jnp.float32)
    change = widened[1:] - widened[:-1]
    position = first_frame - 1 + jnp.arange(change.shape[0], dtype=jnp.int32)
    inside = ((position >= 0) & (position <= frame_total - 2)).astype(jnp.float32)
    normed = inside[:, None, None, None] * (
        change / jnp.sqrt(jnp.sum(change * change, axis=1, keepdims=True) + SMOOTHING)
    )
    return normed[:-1] - normed[1:]


def normed_change(later, earlier, valid):
    change = later.astype(jnp.float32) - earlier.astype(jnp.float32)
    scale = jnp.sqrt(change[0] * change[0] + change[1] * change[1] + SMOOTHING)
    return valid * (change / scale)


def tv_single(images, frame_index, frame_total):
    count = lax.axis_size("frame")
    image = images[0]
    earlier = lax.ppermute(image, "frame", [(i, i + 1) for i in range(count - 1)])
    later = lax.ppermute(image, "frame", [(i + 1, i) for i in range(count - 1)])
    has_earlier = (frame_index >= 1).astype(jnp.float32)
    has_later = (frame_index <= frame_total - 2).astype(jnp.float32)
    return (normed_change(image, earlier, has_earlier) - normed_change(later, image, has_later))[None]


def body(
    images, coil_maps, kspace_data, spoke_angle, band_row, band_col, kernel_rows, kernel_cols
):
    frame_count = images.shape[0]
    extent = images.shape[-1]
    patch_side = kernel_cols.shape[-1]
    coil_count = lax.axis_size("coil")
    coil_index = lax.axis_index("coil")
    rows = extent // coil_count
    transform = transform_table(extent)
    map_rows = exchange_rows(coil_maps[0], rows, coil_count, coil_index)
    first_frame = lax.axis_index("frame") * frame_count
    frame_total = lax.axis_size("frame") * frame_count
    if frame_count == 1:
        tv_grad = tv_single(images, first_frame, frame_total)
    else:
        tv_grad = tv_term(padded(images, (("frame", 0),), 1), first_frame, frame_total)
    row_w = pick_kernels(kernel_rows, spoke_angle[0])
    col_w = pick_kernels(kernel_cols, spoke_angle[0])
    row_select = selector(band_row[0], extent, patch_side)
    col_select = selector(band_col[0], extent, patch_side)
    exact = dict(preferred_element_type=jnp.float32)
    col_placed = jnp.einsum("gjq,gkq->gjk", col_w, col_select, **exact).astype(jnp.bfloat16)
    row_placed = jnp.einsum("grj,gir->gij", row_w, row_select, **exact)
    residual = forward_residual(
        transform, images[0], coil_maps[0], kspace_data[0, 0], row_placed, col_placed
    )
    residuals = jnp.stack(
        [residual] + [rotated(residual, coil_count, shift) for shift in range(1, coil_count)]
    )
    grad_rows = backward_rows(
        transform, residuals, map_rows, row_select, row_w, col_placed, coil_index
    )
    tv_grad, grad_rows = lax.optimization_barrier((tv_grad, grad_rows.astype(jnp.bfloat16)))
    data_grad = lax.all_gather(grad_rows, "coil", axis=1, tiled=True).astype(jnp.float32)[None]
    return images.astype(jnp.float32) - STEP_SIZE * (data_grad + TV_WEIGHT * tv_grad)


def solution(mesh):
    in_specs = (
        P(("grp", "frame"), None, None, None),
        P(("grp", "coil"), None, None, None),
        P(("grp", "frame"), "coil", None, None, None),
        P(("grp", "frame"), None),
        P(("grp", "frame"), None),
        P(("grp", "frame"), None),
        P(),
        P(),
    )
    out_specs = P(("grp", "frame"), None, None, None)
    return jax.shard_map(body, mesh=mesh, in_specs=in_specs, out_specs=out_specs, check_vma=False)
```

```python
import math

import jax
import ml_dtypes
import numpy as np
import jax.numpy as jnp
from jax import lax
from jax.sharding import PartitionSpec as P


SMOOTHING = 0.05
STEP_SIZE = 1.0
TV_WEIGHT = 0.2


def padded(cells, sides, width):
    for axis, dim in sides:
        count = lax.axis_size(axis)
        ends = count - 1
        head = lax.slice_in_dim(cells, 0, width, axis=dim)
        tail = lax.slice_in_dim(cells, cells.shape[dim] - width, cells.shape[dim], axis=dim)
        cells = jnp.concatenate(
            [
                lax.ppermute(tail, axis, [(i, (i + 1) % count) for i in range(ends)]),
                cells,
                lax.ppermute(head, axis, [((i + 1) % count, i) for i in range(ends)]),
            ],
            axis=dim,
        )
    return cells


def transform_table(extent):
    indices = np.arange(extent, dtype=np.int64)
    phases = (indices[:, None] * indices[None, :] % extent).astype(np.float32)
    angle_values = np.float32(2.0 * math.pi / extent) * phases
    scaling = np.float32(1.0 / math.sqrt(extent))
    cos_t = (np.cos(angle_values) * scaling).astype(ml_dtypes.bfloat16)
    sin_t = (np.sin(angle_values) * scaling).astype(ml_dtypes.bfloat16)
    block = np.block([[cos_t, sin_t], [-sin_t, cos_t]])
    block = lax.optimization_barrier(jnp.asarray(block))
    return jnp.stack([block[:extent, :extent], block[:extent, extent:]]), block


def combine_parts(products, direction):
    real_part = products[0, 0] + direction * products[1, 1]
    imaginary = products[0, 1] - direction * products[1, 0]
    return jnp.stack([real_part, imaginary])


def rotated(block, coil_count, shift):
    return lax.ppermute(block, "coil", [(i, (i + shift) % coil_count) for i in range(coil_count)])


def exchange_rows(coil_map, rows, coil_count, coil_index):
    received = [lax.dynamic_slice_in_dim(coil_map, coil_index * rows, rows, axis=1)]
    for shift in range(1, coil_count):
        target = (coil_index + shift) % coil_count
        block = lax.dynamic_slice_in_dim(coil_map, target * rows, rows, axis=1)
        received.append(rotated(block, coil_count, shift))
    return jnp.stack(received)


def selector(first_index, extent, patch_side):
    positions = jnp.arange(extent, dtype=jnp.int32)
    offsets = jnp.arange(patch_side, dtype=jnp.int32)
    wanted = first_index[:, None, None] + offsets[None, None, :]
    return (positions[None, :, None] == wanted).astype(jnp.bfloat16)


def pick_kernels(kernels, angle_ids):
    choice = (angle_ids[:, None] == jnp.arange(kernels.shape[0], dtype=jnp.int32)[None, :])
    flat = kernels.reshape(kernels.shape[0], -1)
    picked = jnp.dot(choice.astype(kernels.dtype), flat, preferred_element_type=jnp.float32)
    return picked.astype(kernels.dtype).reshape((angle_ids.shape[0],) + kernels.shape[1:])


def forward_residual(transform, block, frame_image, coil_map, measured, row_placed, col_placed):
    map_planes = coil_map.astype(jnp.float32)
    image_planes = frame_image.astype(jnp.float32)
    coil_image = jnp.stack(
        [
            map_planes[0] * image_planes[0] - map_planes[1] * image_planes[1],
            map_planes[0] * image_planes[1] + map_planes[1] * image_planes[0],
        ]
    ).astype(jnp.bfloat16)
    products = jnp.einsum(
        "bij,ajk->abik", coil_image, transform, preferred_element_type=jnp.float32
    )
    half_done = combine_parts(products, 1.0).astype(jnp.bfloat16)
    extent = transform.shape[-1]
    kspace = jnp.dot(
        block, half_done.reshape(2 * extent, extent), preferred_element_type=jnp.float32
    ).astype(jnp.bfloat16).reshape(2, extent, extent)
    contracted = jnp.einsum("pik,gjk->pgij", kspace, col_placed, preferred_element_type=jnp.float32)
    predicted = jnp.sum(contracted * row_placed[None], axis=2)
    return predicted - measured


def backward_rows(transform, residuals, map_rows, row_select, row_w, col_placed, coil_index):
    rows = map_rows.shape[2]
    spread = (row_w.astype(jnp.float32)[None, None] * residuals[:, :, :, None, :]).astype(jnp.bfloat16)
    placed = jnp.einsum(
        "cpgrj,gjk->cpgrk", spread, col_placed, preferred_element_type=jnp.float32
    ).astype(jnp.bfloat16)
    row_table = lax.dynamic_slice_in_dim(transform, coil_index * rows, rows, axis=1)
    table_at = jnp.einsum(
        "aij,gjr->aigr", row_table, row_select, preferred_element_type=jnp.float32
    ).astype(jnp.bfloat16)
    products = jnp.einsum("aigr,cbgrk->abcik", table_at, placed, preferred_element_type=jnp.float32)
    half_back = combine_parts(products, -1.0).astype(jnp.bfloat16)
    products = jnp.einsum("bcij,ajk->abcik", half_back, transform, preferred_element_type=jnp.float32)
    coil_back = combine_parts(products, -1.0)
    maps = map_rows.astype(jnp.float32)
    real_part = jnp.sum(maps[:, 0] * coil_back[0] + maps[:, 1] * coil_back[1], axis=0)
    imaginary = jnp.sum(maps[:, 0] * coil_back[1] - maps[:, 1] * coil_back[0], axis=0)
    return jnp.stack([real_part, imaginary])


def tv_term(extended, first_frame, frame_total):
    widened = extended.astype(jnp.float32)
    change = widened[1:] - widened[:-1]
    position = first_frame - 1 + jnp.arange(change.shape[0], dtype=jnp.int32)
    inside = ((position >= 0) & (position <= frame_total - 2)).astype(jnp.float32)
    normed = inside[:, None, None, None] * (
        change / jnp.sqrt(jnp.sum(change * change, axis=1, keepdims=True) + SMOOTHING)
    )
    return normed[:-1] - normed[1:]


def normed_change(later, earlier, valid):
    change = later.astype(jnp.float32) - earlier.astype(jnp.float32)
    scale = jnp.sqrt(change[0] * change[0] + change[1] * change[1] + SMOOTHING)
    return valid * (change / scale)


def tv_single(images, frame_index, frame_total):
    count = lax.axis_size("frame")
    image = images[0]
    earlier = lax.ppermute(image, "frame", [(i, i + 1) for i in range(count - 1)])
    later = lax.ppermute(image, "frame", [(i + 1, i) for i in range(count - 1)])
    has_earlier = (frame_index >= 1).astype(jnp.float32)
    has_later = (frame_index <= frame_total - 2).astype(jnp.float32)
    return (
        normed_change(image, earlier, has_earlier) - normed_change(later, image, has_later)
    )[None]


def body(
    images, coil_maps, kspace_data, spoke_angle, band_row, band_col, kernel_rows, kernel_cols
):
    frame_count = images.shape[0]
    extent = images.shape[-1]
    patch_side = kernel_cols.shape[-1]
    coil_count = lax.axis_size("coil")
    coil_index = lax.axis_index("coil")
    rows = extent // coil_count
    transform, block = transform_table(extent)
    map_rows = exchange_rows(coil_maps[0], rows, coil_count, coil_index)
    first_frame = lax.axis_index("frame") * frame_count
    frame_total = lax.axis_size("frame") * frame_count
    if frame_count == 1:
        tv_grad = tv_single(images, first_frame, frame_total)
    else:
        tv_grad = tv_term(padded(images, (("frame", 0),), 1), first_frame, frame_total)
    row_w = pick_kernels(kernel_rows, spoke_angle[0])
    col_w = pick_kernels(kernel_cols, spoke_angle[0])
    row_select = selector(band_row[0], extent, patch_side)
    col_select = selector(band_col[0], extent, patch_side)
    exact = dict(preferred_element_type=jnp.float32)
    col_placed = jnp.einsum("gjq,gkq->gjk", col_w, col_select, **exact).astype(jnp.bfloat16)
    row_placed = jnp.einsum("grj,gir->gij", row_w, row_select, **exact)
    residual = forward_residual(
        transform, block, images[0], coil_maps[0], kspace_data[0, 0], row_placed, col_placed
    )
    moved = [rotated(residual, coil_count, shift) for shift in range(1, coil_count)]
    residuals = jnp.stack([residual] + moved)
    grad_rows = backward_rows(
        transform, residuals, map_rows, row_select, row_w, col_placed, coil_index
    )
    tv_grad, grad_rows = lax.optimization_barrier((tv_grad, grad_rows.astype(jnp.bfloat16)))
    data_grad = lax.all_gather(grad_rows, "coil", axis=1, tiled=True).astype(jnp.float32)[None]
    return images.astype(jnp.float32) - STEP_SIZE * (data_grad + TV_WEIGHT * tv_grad)


def solution(mesh):
    in_specs = (
        P(("grp", "frame"), None, None, None),
        P(("grp", "coil"), None, None, None),
        P(("grp", "frame"), "coil", None, None, None),
        P(("grp", "frame"), None),
        P(("grp", "frame"), None),
        P(("grp", "frame"), None),
        P(),
        P(),
    )
    out_specs = P(("grp", "frame"), None, None, None)
    return jax.shard_map(body, mesh=mesh, in_specs=in_specs, out_specs=out_specs, check_vma=False)
```

```python
import math

import jax
import ml_dtypes
import numpy as np
import jax.numpy as jnp
from jax import lax
from jax.sharding import PartitionSpec as P


SMOOTHING = 0.05
STEP_SIZE = 1.0
TV_WEIGHT = 0.2


def padded(cells, sides, width):
    for axis, dim in sides:
        count = lax.axis_size(axis)
        ends = count - 1
        head = lax.slice_in_dim(cells, 0, width, axis=dim)
        tail = lax.slice_in_dim(cells, cells.shape[dim] - width, cells.shape[dim], axis=dim)
        cells = jnp.concatenate(
            [
                lax.ppermute(tail, axis, [(i, (i + 1) % count) for i in range(ends)]),
                cells,
                lax.ppermute(head, axis, [((i + 1) % count, i) for i in range(ends)]),
            ],
            axis=dim,
        )
    return cells


def transform_table(extent):
    indices = np.arange(extent, dtype=np.int64)
    phases = (indices[:, None] * indices[None, :] % extent).astype(np.float32)
    angle_values = np.float32(2.0 * math.pi / extent) * phases
    scaling = np.float32(1.0 / math.sqrt(extent))
    table = np.stack([np.cos(angle_values) * scaling, np.sin(angle_values) * scaling])
    return jnp.asarray(table.astype(ml_dtypes.bfloat16))


def combine_parts(products, direction):
    real_part = products[0, 0] + direction * products[1, 1]
    imaginary = products[0, 1] - direction * products[1, 0]
    return jnp.stack([real_part, imaginary])


def rotated(block, coil_count, shift):
    return lax.ppermute(block, "coil", [(i, (i + shift) % coil_count) for i in range(coil_count)])


def exchange_rows(coil_map, rows, coil_count, coil_index):
    received = [lax.dynamic_slice_in_dim(coil_map, coil_index * rows, rows, axis=1)]
    for shift in range(1, coil_count):
        target = (coil_index + shift) % coil_count
        block = lax.dynamic_slice_in_dim(coil_map, target * rows, rows, axis=1)
        received.append(rotated(block, coil_count, shift))
    return jnp.stack(received)


def selector(first_index, extent, patch_side):
    positions = jnp.arange(extent, dtype=jnp.int32)
    offsets = jnp.arange(patch_side, dtype=jnp.int32)
    wanted = first_index[:, None, None] + offsets[None, None, :]
    return (positions[None, :, None] == wanted).astype(jnp.bfloat16)


def pick_kernels(kernels, angle_ids):
    choice = (angle_ids[:, None] == jnp.arange(kernels.shape[0], dtype=jnp.int32)[None, :])
    flat = kernels.reshape(kernels.shape[0], -1)
    picked = jnp.dot(choice.astype(kernels.dtype), flat, preferred_element_type=jnp.float32)
    return picked.astype(kernels.dtype).reshape((angle_ids.shape[0],) + kernels.shape[1:])


def forward_residual(transform, frame_image, coil_map, measured, row_placed, col_placed):
    map_planes = coil_map.astype(jnp.float32)
    image_planes = frame_image.astype(jnp.float32)
    coil_image = jnp.stack(
        [
            map_planes[0] * image_planes[0] - map_planes[1] * image_planes[1],
            map_planes[0] * image_planes[1] + map_planes[1] * image_planes[0],
        ]
    ).astype(jnp.bfloat16)
    products = jnp.einsum(
        "bij,ajk->abik", coil_image, transform, preferred_element_type=jnp.float32
    )
    half_done = combine_parts(products, 1.0).astype(jnp.bfloat16)
    cos_t, sin_t = lax.optimization_barrier(transform)
    block = jnp.concatenate(
        [jnp.concatenate([cos_t, sin_t], axis=1), jnp.concatenate([-sin_t, cos_t], axis=1)]
    )
    extent = transform.shape[-1]
    kspace = jnp.dot(
        block, half_done.reshape(2 * extent, extent), preferred_element_type=jnp.float32
    ).astype(jnp.bfloat16).reshape(2, extent, extent)
    contracted = jnp.einsum("pik,gjk->pgij", kspace, col_placed, preferred_element_type=jnp.float32)
    predicted = jnp.sum(contracted * row_placed[None], axis=2)
    return predicted - measured


def backward_rows(transform, residuals, map_rows, row_select, row_w, col_placed, coil_index):
    rows = map_rows.shape[2]
    spread = (row_w.astype(jnp.float32)[None, None] * residuals[:, :, :, None, :]).astype(jnp.bfloat16)
    placed = jnp.einsum(
        "cpgrj,gjk->cpgrk", spread, col_placed, preferred_element_type=jnp.float32
    ).astype(jnp.bfloat16)
    row_table = lax.dynamic_slice_in_dim(transform, coil_index * rows, rows, axis=1)
    table_at = jnp.einsum(
        "aij,gjr->aigr", row_table, row_select, preferred_element_type=jnp.float32
    ).astype(jnp.bfloat16)
    products = jnp.einsum("aigr,cbgrk->abcik", table_at, placed, preferred_element_type=jnp.float32)
    half_back = combine_parts(products, -1.0).astype(jnp.bfloat16)
    products = jnp.einsum("bcij,ajk->abcik", half_back, transform, preferred_element_type=jnp.float32)
    coil_back = combine_parts(products, -1.0)
    maps = map_rows.astype(jnp.float32)
    real_part = jnp.sum(maps[:, 0] * coil_back[0] + maps[:, 1] * coil_back[1], axis=0)
    imaginary = jnp.sum(maps[:, 0] * coil_back[1] - maps[:, 1] * coil_back[0], axis=0)
    return jnp.stack([real_part, imaginary])


def tv_term(extended, first_frame, frame_total):
    widened = extended.astype(jnp.float32)
    change = widened[1:] - widened[:-1]
    position = first_frame - 1 + jnp.arange(change.shape[0], dtype=jnp.int32)
    inside = ((position >= 0) & (position <= frame_total - 2)).astype(jnp.float32)
    normed = inside[:, None, None, None] * (
        change / jnp.sqrt(jnp.sum(change * change, axis=1, keepdims=True) + SMOOTHING)
    )
    return normed[:-1] - normed[1:]


def normed_change(later, earlier, valid):
    change = later.astype(jnp.float32) - earlier.astype(jnp.float32)
    scale = jnp.sqrt(change[0] * change[0] + change[1] * change[1] + SMOOTHING)
    return valid * (change / scale)


def tv_single(images, frame_index, frame_total):
    count = lax.axis_size("frame")
    image = images[0]
    earlier = lax.ppermute(image, "frame", [(i, i + 1) for i in range(count - 1)])
    later = lax.ppermute(image, "frame", [(i + 1, i) for i in range(count - 1)])
    has_earlier = (frame_index >= 1).astype(jnp.float32)
    has_later = (frame_index <= frame_total - 2).astype(jnp.float32)
    return (
        normed_change(image, earlier, has_earlier) - normed_change(later, image, has_later)
    )[None]


def body(
    images, coil_maps, kspace_data, spoke_angle, band_row, band_col, kernel_rows, kernel_cols
):
    frame_count = images.shape[0]
    extent = images.shape[-1]
    patch_side = kernel_cols.shape[-1]
    coil_count = lax.axis_size("coil")
    coil_index = lax.axis_index("coil")
    rows = extent // coil_count
    transform = transform_table(extent)
    map_rows = exchange_rows(coil_maps[0], rows, coil_count, coil_index)
    first_frame = lax.axis_index("frame") * frame_count
    frame_total = lax.axis_size("frame") * frame_count
    if frame_count == 1:
        tv_grad = tv_single(images, first_frame, frame_total)
    else:
        tv_grad = tv_term(padded(images, (("frame", 0),), 1), first_frame, frame_total)
    row_w = pick_kernels(kernel_rows, spoke_angle[0])
    col_w = pick_kernels(kernel_cols, spoke_angle[0])
    row_select = selector(band_row[0], extent, patch_side)
    col_select = selector(band_col[0], extent, patch_side)
    exact = dict(preferred_element_type=jnp.float32)
    col_placed = jnp.einsum("gjq,gkq->gjk", col_w, col_select, **exact).astype(jnp.bfloat16)
    row_placed = jnp.einsum("grj,gir->gij", row_w, row_select, **exact)
    residual = forward_residual(
        transform, images[0], coil_maps[0], kspace_data[0, 0], row_placed, col_placed
    )
    moved = [rotated(residual, coil_count, shift) for shift in range(1, coil_count)]
    residuals = jnp.stack([residual] + moved)
    grad_rows = backward_rows(
        transform, residuals, map_rows, row_select, row_w, col_placed, coil_index
    )
    tv_grad, grad_rows = lax.optimization_barrier((tv_grad, grad_rows.astype(jnp.bfloat16)))
    data_grad = lax.all_gather(grad_rows, "coil", axis=1, tiled=True).astype(jnp.float32)[None]
    return images.astype(jnp.float32) - STEP_SIZE * (data_grad + TV_WEIGHT * tv_grad)


def solution(mesh):
    in_specs = (
        P(("grp", "frame"), None, None, None),
        P(("grp", "coil"), None, None, None),
        P(("grp", "frame"), "coil", None, None, None),
        P(("grp", "frame"), None),
        P(("grp", "frame"), None),
        P(("grp", "frame"), None),
        P(),
        P(),
    )
    out_specs = P(("grp", "frame"), None, None, None)
    return jax.shard_map(body, mesh=mesh, in_specs=in_specs, out_specs=out_specs, check_vma=False)
```

```python
import math

import jax
import ml_dtypes
import numpy as np
import jax.numpy as jnp
from jax import lax
from jax.sharding import PartitionSpec as P


SMOOTHING = 0.05
STEP_SIZE = 1.0
TV_WEIGHT = 0.2


def padded(cells, sides, width):
    for axis, dim in sides:
        count = lax.axis_size(axis)
        ends = count - 1
        head = lax.slice_in_dim(cells, 0, width, axis=dim)
        tail = lax.slice_in_dim(cells, cells.shape[dim] - width, cells.shape[dim], axis=dim)
        cells = jnp.concatenate(
            [
                lax.ppermute(tail, axis, [(i, (i + 1) % count) for i in range(ends)]),
                cells,
                lax.ppermute(head, axis, [((i + 1) % count, i) for i in range(ends)]),
            ],
            axis=dim,
        )
    return cells


def transform_table(extent):
    indices = np.arange(extent, dtype=np.int64)
    phases = (indices[:, None] * indices[None, :] % extent).astype(np.float32)
    angle_values = np.float32(2.0 * math.pi / extent) * phases
    scaling = np.float32(1.0 / math.sqrt(extent))
    cos_t = (np.cos(angle_values) * scaling).astype(ml_dtypes.bfloat16)
    sin_t = (np.sin(angle_values) * scaling).astype(ml_dtypes.bfloat16)
    return lax.optimization_barrier(jnp.asarray(np.block([[cos_t, sin_t], [-sin_t, cos_t]])))


def combine_parts(products, direction):
    real_part = products[0, 0] + direction * products[1, 1]
    imaginary = products[0, 1] - direction * products[1, 0]
    return jnp.stack([real_part, imaginary])


def rotated(block, coil_count, shift):
    return lax.ppermute(block, "coil", [(i, (i + shift) % coil_count) for i in range(coil_count)])


def exchange_rows(coil_map, rows, coil_count, coil_index):
    received = [lax.dynamic_slice_in_dim(coil_map, coil_index * rows, rows, axis=1)]
    for shift in range(1, coil_count):
        target = (coil_index + shift) % coil_count
        block = lax.dynamic_slice_in_dim(coil_map, target * rows, rows, axis=1)
        received.append(rotated(block, coil_count, shift))
    return jnp.stack(received)


def selector(first_index, extent, patch_side):
    positions = jnp.arange(extent, dtype=jnp.int32)
    offsets = jnp.arange(patch_side, dtype=jnp.int32)
    wanted = first_index[:, None, None] + offsets[None, None, :]
    return (positions[None, :, None] == wanted).astype(jnp.bfloat16)


def pick_kernels(kernels, angle_ids):
    choice = (angle_ids[:, None] == jnp.arange(kernels.shape[0], dtype=jnp.int32)[None, :])
    flat = kernels.reshape(kernels.shape[0], -1)
    picked = jnp.dot(choice.astype(kernels.dtype), flat, preferred_element_type=jnp.float32)
    return picked.astype(kernels.dtype).reshape((angle_ids.shape[0],) + kernels.shape[1:])


def forward_residual(block, frame_image, coil_map, measured, row_placed, col_placed):
    map_planes = coil_map.astype(jnp.float32)
    image_planes = frame_image.astype(jnp.float32)
    coil_image = jnp.stack(
        [
            map_planes[0] * image_planes[0] - map_planes[1] * image_planes[1],
            map_planes[0] * image_planes[1] + map_planes[1] * image_planes[0],
        ]
    ).astype(jnp.bfloat16)
    extent = block.shape[0] // 2
    side = block[:extent]
    out = jnp.dot(
        coil_image.reshape(2 * extent, extent), side, preferred_element_type=jnp.float32
    ).reshape(2, extent, 2, extent)
    half_done = jnp.stack(
        [out[0, :, 0] + out[1, :, 1], out[1, :, 0] - out[0, :, 1]]
    ).astype(jnp.bfloat16)
    kspace = jnp.dot(
        block, half_done.reshape(2 * extent, extent), preferred_element_type=jnp.float32
    ).astype(jnp.bfloat16).reshape(2, extent, extent)
    contracted = jnp.einsum("pik,gjk->pgij", kspace, col_placed, preferred_element_type=jnp.float32)
    predicted = jnp.sum(contracted * row_placed[None], axis=2)
    return predicted - measured


def backward_rows(block, residuals, map_rows, row_select, row_w, col_placed, coil_index):
    rows = map_rows.shape[2]
    spread = (row_w.astype(jnp.float32)[None, None] * residuals[:, :, :, None, :]).astype(jnp.bfloat16)
    placed = jnp.einsum(
        "cpgrj,gjk->cpgrk", spread, col_placed, preferred_element_type=jnp.float32
    ).astype(jnp.bfloat16)
    extent = block.shape[0] // 2
    row_table = lax.dynamic_slice_in_dim(block[:extent], coil_index * rows, rows, axis=0)
    table_at = jnp.einsum(
        "iaj,gjr->aigr", row_table.reshape(rows, 2, extent), row_select,
        preferred_element_type=jnp.float32,
    ).astype(jnp.bfloat16)
    products = jnp.einsum("aigr,cbgrk->abcik", table_at, placed, preferred_element_type=jnp.float32)
    half_back = combine_parts(products, -1.0).astype(jnp.bfloat16)
    planes, coil_count = half_back.shape[:2]
    out = jnp.dot(
        half_back.reshape(planes * coil_count * rows, extent), block[:extent],
        preferred_element_type=jnp.float32,
    ).reshape(planes, coil_count, rows, 2, extent)
    coil_back = jnp.stack(
        [out[0, :, :, 0] - out[1, :, :, 1], out[1, :, :, 0] + out[0, :, :, 1]]
    )
    maps = map_rows.astype(jnp.float32)
    real_part = jnp.sum(maps[:, 0] * coil_back[0] + maps[:, 1] * coil_back[1], axis=0)
    imaginary = jnp.sum(maps[:, 0] * coil_back[1] - maps[:, 1] * coil_back[0], axis=0)
    return jnp.stack([real_part, imaginary])


def tv_term(extended, first_frame, frame_total):
    widened = extended.astype(jnp.float32)
    change = widened[1:] - widened[:-1]
    position = first_frame - 1 + jnp.arange(change.shape[0], dtype=jnp.int32)
    inside = ((position >= 0) & (position <= frame_total - 2)).astype(jnp.float32)
    normed = inside[:, None, None, None] * (
        change / jnp.sqrt(jnp.sum(change * change, axis=1, keepdims=True) + SMOOTHING)
    )
    return normed[:-1] - normed[1:]


def normed_change(later, earlier, valid):
    change = later.astype(jnp.float32) - earlier.astype(jnp.float32)
    scale = jnp.sqrt(change[0] * change[0] + change[1] * change[1] + SMOOTHING)
    return valid * (change / scale)


def tv_single(images, frame_index, frame_total):
    count = lax.axis_size("frame")
    image = images[0]
    earlier = lax.ppermute(image, "frame", [(i, i + 1) for i in range(count - 1)])
    later = lax.ppermute(image, "frame", [(i + 1, i) for i in range(count - 1)])
    has_earlier = (frame_index >= 1).astype(jnp.float32)
    has_later = (frame_index <= frame_total - 2).astype(jnp.float32)
    return (normed_change(image, earlier, has_earlier) - normed_change(later, image, has_later))[None]


def body(
    images, coil_maps, kspace_data, spoke_angle, band_row, band_col, kernel_rows, kernel_cols
):
    frame_count = images.shape[0]
    extent = images.shape[-1]
    patch_side = kernel_cols.shape[-1]
    coil_count = lax.axis_size("coil")
    coil_index = lax.axis_index("coil")
    rows = extent // coil_count
    block = transform_table(extent)
    map_rows = exchange_rows(coil_maps[0], rows, coil_count, coil_index)
    first_frame = lax.axis_index("frame") * frame_count
    frame_total = lax.axis_size("frame") * frame_count
    if frame_count == 1:
        tv_grad = tv_single(images, first_frame, frame_total)
    else:
        tv_grad = tv_term(padded(images, (("frame", 0),), 1), first_frame, frame_total)
    row_w = pick_kernels(kernel_rows, spoke_angle[0])
    col_w = pick_kernels(kernel_cols, spoke_angle[0])
    row_select = selector(band_row[0], extent, patch_side)
    col_select = selector(band_col[0], extent, patch_side)
    exact = dict(preferred_element_type=jnp.float32)
    col_placed = jnp.einsum("gjq,gkq->gjk", col_w, col_select, **exact).astype(jnp.bfloat16)
    row_placed = jnp.einsum("grj,gir->gij", row_w, row_select, **exact)
    residual = forward_residual(
        block, images[0], coil_maps[0], kspace_data[0, 0], row_placed, col_placed
    )
    residuals = jnp.stack(
        [residual] + [rotated(residual, coil_count, shift) for shift in range(1, coil_count)]
    )
    grad_rows = backward_rows(
        block, residuals, map_rows, row_select, row_w, col_placed, coil_index
    )
    tv_grad, grad_rows = lax.optimization_barrier((tv_grad, grad_rows.astype(jnp.bfloat16)))
    data_grad = lax.all_gather(grad_rows, "coil", axis=1, tiled=True).astype(jnp.float32)[None]
    return images.astype(jnp.float32) - STEP_SIZE * (data_grad + TV_WEIGHT * tv_grad)


def solution(mesh):
    in_specs = (
        P(("grp", "frame"), None, None, None),
        P(("grp", "coil"), None, None, None),
        P(("grp", "frame"), "coil", None, None, None),
        P(("grp", "frame"), None),
        P(("grp", "frame"), None),
        P(("grp", "frame"), None),
        P(),
        P(),
    )
    out_specs = P(("grp", "frame"), None, None, None)
    return jax.shard_map(body, mesh=mesh, in_specs=in_specs, out_specs=out_specs, check_vma=False)
```

```python
import math

import jax
import ml_dtypes
import numpy as np
import jax.numpy as jnp
from jax import lax
from jax.sharding import PartitionSpec as P


SMOOTHING = 0.05
STEP_SIZE = 1.0
TV_WEIGHT = 0.2


def padded(cells, sides, width):
    for axis, dim in sides:
        count = lax.axis_size(axis)
        ends = count - 1
        head = lax.slice_in_dim(cells, 0, width, axis=dim)
        tail = lax.slice_in_dim(cells, cells.shape[dim] - width, cells.shape[dim], axis=dim)
        cells = jnp.concatenate(
            [
                lax.ppermute(tail, axis, [(i, (i + 1) % count) for i in range(ends)]),
                cells,
                lax.ppermute(head, axis, [((i + 1) % count, i) for i in range(ends)]),
            ],
            axis=dim,
        )
    return cells


def transform_table(extent):
    indices = np.arange(extent, dtype=np.int64)
    phases = (indices[:, None] * indices[None, :] % extent).astype(np.float32)
    angle_values = np.float32(2.0 * math.pi / extent) * phases
    scaling = np.float32(1.0 / math.sqrt(extent))
    table = np.stack([np.cos(angle_values) * scaling, np.sin(angle_values) * scaling])
    return jnp.asarray(table.astype(ml_dtypes.bfloat16))


def combine_parts(products, direction):
    real_part = products[0, 0] + direction * products[1, 1]
    imaginary = products[0, 1] - direction * products[1, 0]
    return jnp.stack([real_part, imaginary])


def rotated(block, coil_count, shift):
    return lax.ppermute(block, "coil", [(i, (i + shift) % coil_count) for i in range(coil_count)])


def exchange_rows(coil_map, rows, coil_count, coil_index):
    received = [lax.dynamic_slice_in_dim(coil_map, coil_index * rows, rows, axis=1)]
    for shift in range(1, coil_count):
        target = (coil_index + shift) % coil_count
        block = lax.dynamic_slice_in_dim(coil_map, target * rows, rows, axis=1)
        received.append(rotated(block, coil_count, shift))
    return jnp.stack(received)


def exchange_all(image, coil_map, rows, coil_count, coil_index, frame_count):
    extent = image.shape[-1]

    def flat(f, c):
        return f * coil_count + c

    def block_for(shift):
        target = (coil_index + shift) % coil_count
        return lax.dynamic_slice_in_dim(coil_map, target * rows, rows, axis=1)

    def carried(frame_step, coil_step):
        pairs = [
            (flat(f, c), flat((f + frame_step) % frame_count, (c + coil_step) % coil_count))
            for f in range(frame_count)
            for c in range(coil_count)
        ]
        payload = jnp.concatenate([image, block_for(coil_step % coil_count)], axis=1)
        moved = lax.ppermute(payload, ("frame", "coil"), pairs)
        return moved[:, :extent], moved[:, extent:]

    received = [None] * coil_count
    received[0] = block_for(0)
    earlier, received[1] = carried(1, 1)
    later, received[coil_count - 1] = carried(-1, -1)
    for shift in range(2, coil_count - 1):
        received[shift] = rotated(block_for(shift), coil_count, shift)
    return earlier, later, jnp.stack(received)


def tv_from(image, earlier, later, frame_index, frame_total):
    has_earlier = (frame_index >= 1).astype(jnp.float32)
    has_later = (frame_index <= frame_total - 2).astype(jnp.float32)
    return (normed_change(image, earlier, has_earlier) - normed_change(later, image, has_later))[None]


def selector(first_index, extent, patch_side):
    positions = jnp.arange(extent, dtype=jnp.int32)
    offsets = jnp.arange(patch_side, dtype=jnp.int32)
    wanted = first_index[:, None, None] + offsets[None, None, :]
    return (positions[None, :, None] == wanted).astype(jnp.bfloat16)


def pick_kernels(kernels, angle_ids):
    choice = (angle_ids[:, None] == jnp.arange(kernels.shape[0], dtype=jnp.int32)[None, :])
    flat = kernels.reshape(kernels.shape[0], -1)
    picked = jnp.dot(choice.astype(kernels.dtype), flat, preferred_element_type=jnp.float32)
    return picked.astype(kernels.dtype).reshape((angle_ids.shape[0],) + kernels.shape[1:])


def forward_residual(transform, frame_image, coil_map, measured, row_placed, col_placed):
    map_planes = coil_map.astype(jnp.float32)
    image_planes = frame_image.astype(jnp.float32)
    coil_image = jnp.stack(
        [
            map_planes[0] * image_planes[0] - map_planes[1] * image_planes[1],
            map_planes[0] * image_planes[1] + map_planes[1] * image_planes[0],
        ]
    ).astype(jnp.bfloat16)
    products = jnp.einsum(
        "bij,ajk->abik", coil_image, transform, preferred_element_type=jnp.float32
    )
    half_done = combine_parts(products, 1.0).astype(jnp.bfloat16)
    cos_t, sin_t = lax.optimization_barrier(transform)
    block = jnp.concatenate(
        [jnp.concatenate([cos_t, sin_t], axis=1), jnp.concatenate([-sin_t, cos_t], axis=1)]
    )
    extent = transform.shape[-1]
    kspace = jnp.dot(
        block, half_done.reshape(2 * extent, extent), preferred_element_type=jnp.float32
    ).astype(jnp.bfloat16).reshape(2, extent, extent)
    contracted = jnp.einsum("pik,gjk->pgij", kspace, col_placed, preferred_element_type=jnp.float32)
    predicted = jnp.sum(contracted * row_placed[None], axis=2)
    return predicted - measured


def backward_rows(transform, residuals, map_rows, row_select, row_w, col_placed, coil_index):
    rows = map_rows.shape[2]
    spread = (row_w.astype(jnp.float32)[None, None] * residuals[:, :, :, None, :]).astype(jnp.bfloat16)
    placed = jnp.einsum(
        "cpgrj,gjk->cpgrk", spread, col_placed, preferred_element_type=jnp.float32
    ).astype(jnp.bfloat16)
    row_table = lax.dynamic_slice_in_dim(transform, coil_index * rows, rows, axis=1)
    table_at = jnp.einsum(
        "aij,gjr->aigr", row_table, row_select, preferred_element_type=jnp.float32
    ).astype(jnp.bfloat16)
    products = jnp.einsum("aigr,cbgrk->abcik", table_at, placed, preferred_element_type=jnp.float32)
    half_back = combine_parts(products, -1.0).astype(jnp.bfloat16)
    products = jnp.einsum("bcij,ajk->abcik", half_back, transform, preferred_element_type=jnp.float32)
    coil_back = combine_parts(products, -1.0)
    maps = map_rows.astype(jnp.float32)
    real_part = jnp.sum(maps[:, 0] * coil_back[0] + maps[:, 1] * coil_back[1], axis=0)
    imaginary = jnp.sum(maps[:, 0] * coil_back[1] - maps[:, 1] * coil_back[0], axis=0)
    return jnp.stack([real_part, imaginary])


def tv_term(extended, first_frame, frame_total):
    widened = extended.astype(jnp.float32)
    change = widened[1:] - widened[:-1]
    position = first_frame - 1 + jnp.arange(change.shape[0], dtype=jnp.int32)
    inside = ((position >= 0) & (position <= frame_total - 2)).astype(jnp.float32)
    normed = inside[:, None, None, None] * (
        change / jnp.sqrt(jnp.sum(change * change, axis=1, keepdims=True) + SMOOTHING)
    )
    return normed[:-1] - normed[1:]


def normed_change(later, earlier, valid):
    change = later.astype(jnp.float32) - earlier.astype(jnp.float32)
    scale = jnp.sqrt(change[0] * change[0] + change[1] * change[1] + SMOOTHING)
    return valid * (change / scale)


def tv_single(images, frame_index, frame_total):
    count = lax.axis_size("frame")
    image = images[0]
    earlier = lax.ppermute(image, "frame", [(i, i + 1) for i in range(count - 1)])
    later = lax.ppermute(image, "frame", [(i + 1, i) for i in range(count - 1)])
    has_earlier = (frame_index >= 1).astype(jnp.float32)
    has_later = (frame_index <= frame_total - 2).astype(jnp.float32)
    return (normed_change(image, earlier, has_earlier) - normed_change(later, image, has_later))[None]


def body(
    images, coil_maps, kspace_data, spoke_angle, band_row, band_col, kernel_rows, kernel_cols
):
    frame_count = images.shape[0]
    extent = images.shape[-1]
    patch_side = kernel_cols.shape[-1]
    coil_count = lax.axis_size("coil")
    coil_index = lax.axis_index("coil")
    rows = extent // coil_count
    transform = transform_table(extent)
    first_frame = lax.axis_index("frame") * frame_count
    frame_total = lax.axis_size("frame") * frame_count
    if frame_count == 1 and coil_count >= 3:
        earlier, later, map_rows = exchange_all(
            images[0], coil_maps[0], rows, coil_count, coil_index,
            lax.axis_size("frame"),
        )
        tv_grad = tv_from(images[0], earlier, later, first_frame, frame_total)
    else:
        map_rows = exchange_rows(coil_maps[0], rows, coil_count, coil_index)
        if frame_count == 1:
            tv_grad = tv_single(images, first_frame, frame_total)
        else:
            tv_grad = tv_term(padded(images, (("frame", 0),), 1), first_frame, frame_total)
    row_w = pick_kernels(kernel_rows, spoke_angle[0])
    col_w = pick_kernels(kernel_cols, spoke_angle[0])
    row_select = selector(band_row[0], extent, patch_side)
    col_select = selector(band_col[0], extent, patch_side)
    exact = dict(preferred_element_type=jnp.float32)
    col_placed = jnp.einsum("gjq,gkq->gjk", col_w, col_select, **exact).astype(jnp.bfloat16)
    row_placed = jnp.einsum("grj,gir->gij", row_w, row_select, **exact)
    residual = forward_residual(
        transform, images[0], coil_maps[0], kspace_data[0, 0], row_placed, col_placed
    )
    residuals = jnp.stack(
        [residual] + [rotated(residual, coil_count, shift) for shift in range(1, coil_count)]
    )
    grad_rows = backward_rows(
        transform, residuals, map_rows, row_select, row_w, col_placed, coil_index
    )
    tv_grad, grad_rows = lax.optimization_barrier((tv_grad, grad_rows.astype(jnp.bfloat16)))
    data_grad = lax.all_gather(grad_rows, "coil", axis=1, tiled=True).astype(jnp.float32)[None]
    return images.astype(jnp.float32) - STEP_SIZE * (data_grad + TV_WEIGHT * tv_grad)


def solution(mesh):
    in_specs = (
        P(("grp", "frame"), None, None, None),
        P(("grp", "coil"), None, None, None),
        P(("grp", "frame"), "coil", None, None, None),
        P(("grp", "frame"), None),
        P(("grp", "frame"), None),
        P(("grp", "frame"), None),
        P(),
        P(),
    )
    out_specs = P(("grp", "frame"), None, None, None)
    return jax.shard_map(body, mesh=mesh, in_specs=in_specs, out_specs=out_specs, check_vma=False)
```

```python
import math

import jax
import ml_dtypes
import numpy as np
import jax.numpy as jnp
from jax import lax
from jax.sharding import PartitionSpec as P


SMOOTHING = 0.05
STEP_SIZE = 1.0
TV_WEIGHT = 0.2


def padded(cells, sides, width):
    for axis, dim in sides:
        count = lax.axis_size(axis)
        ends = count - 1
        head = lax.slice_in_dim(cells, 0, width, axis=dim)
        tail = lax.slice_in_dim(cells, cells.shape[dim] - width, cells.shape[dim], axis=dim)
        cells = jnp.concatenate(
            [
                lax.ppermute(tail, axis, [(i, (i + 1) % count) for i in range(ends)]),
                cells,
                lax.ppermute(head, axis, [((i + 1) % count, i) for i in range(ends)]),
            ],
            axis=dim,
        )
    return cells


def transform_table(extent):
    indices = np.arange(extent, dtype=np.int64)
    phases = (indices[:, None] * indices[None, :] % extent).astype(np.float32)
    angle_values = np.float32(2.0 * math.pi / extent) * phases
    scaling = np.float32(1.0 / math.sqrt(extent))
    table = np.stack([np.cos(angle_values) * scaling, np.sin(angle_values) * scaling])
    return jnp.asarray(table.astype(ml_dtypes.bfloat16))


def combine_parts(products, direction):
    real_part = products[0, 0] + direction * products[1, 1]
    imaginary = products[0, 1] - direction * products[1, 0]
    return jnp.stack([real_part, imaginary])


def rotated(block, coil_count, shift):
    return lax.ppermute(block, "coil", [(i, (i + shift) % coil_count) for i in range(coil_count)])


def exchange_rows(coil_map, rows, coil_count, coil_index):
    received = [lax.dynamic_slice_in_dim(coil_map, coil_index * rows, rows, axis=1)]
    for shift in range(1, coil_count):
        target = (coil_index + shift) % coil_count
        block = lax.dynamic_slice_in_dim(coil_map, target * rows, rows, axis=1)
        received.append(rotated(block, coil_count, shift))
    return jnp.stack(received)


def selector(first_index, extent, patch_side):
    positions = jnp.arange(extent, dtype=jnp.int32)
    offsets = jnp.arange(patch_side, dtype=jnp.int32)
    wanted = first_index[:, None, None] + offsets[None, None, :]
    return (positions[None, :, None] == wanted).astype(jnp.bfloat16)


def pick_kernels(kernels, angle_ids):
    choice = (angle_ids[:, None] == jnp.arange(kernels.shape[0], dtype=jnp.int32)[None, :])
    flat = kernels.reshape(kernels.shape[0], -1)
    picked = jnp.dot(choice.astype(kernels.dtype), flat, preferred_element_type=jnp.float32)
    return picked.astype(kernels.dtype).reshape((angle_ids.shape[0],) + kernels.shape[1:])


def forward_residual(transform, frame_image, coil_map, measured, row_placed, col_placed):
    map_planes = coil_map.astype(jnp.float32)
    image_planes = frame_image.astype(jnp.float32)
    coil_image = jnp.stack(
        [
            map_planes[0] * image_planes[0] - map_planes[1] * image_planes[1],
            map_planes[0] * image_planes[1] + map_planes[1] * image_planes[0],
        ]
    ).astype(jnp.bfloat16)
    products = jnp.einsum(
        "bij,ajk->abik", coil_image, transform, preferred_element_type=jnp.float32
    )
    half_done = combine_parts(products, 1.0).astype(jnp.bfloat16)
    cos_t, sin_t = lax.optimization_barrier(transform)
    block = jnp.concatenate(
        [jnp.concatenate([cos_t, sin_t], axis=1), jnp.concatenate([-sin_t, cos_t], axis=1)]
    )
    extent = transform.shape[-1]
    kspace = jnp.dot(
        block, half_done.reshape(2 * extent, extent), preferred_element_type=jnp.float32
    ).astype(jnp.bfloat16).reshape(2, extent, extent)
    contracted = jnp.einsum("pik,gjk->pgij", kspace, col_placed, preferred_element_type=jnp.float32)
    predicted = jnp.sum(contracted * row_placed[None], axis=2)
    return predicted - measured


def backward_rows(transform, residuals, map_rows, row_select, row_w, col_placed, coil_index):
    rows = map_rows.shape[2]
    row_table = lax.dynamic_slice_in_dim(transform, coil_index * rows, rows, axis=1)
    table_at = jnp.einsum(
        "aij,gjr->aigr", row_table, row_select, preferred_element_type=jnp.float32
    ).astype(jnp.bfloat16)
    halves = []
    for source in range(residuals.shape[0]):
        spread = (row_w.astype(jnp.float32)[None] * residuals[source][:, :, None, :]).astype(
            jnp.bfloat16
        )
        placed = jnp.einsum(
            "pgrj,gjk->pgrk", spread, col_placed, preferred_element_type=jnp.float32
        ).astype(jnp.bfloat16)
        products = jnp.einsum(
            "aigr,bgrk->abik", table_at, placed, preferred_element_type=jnp.float32
        )
        halves.append(combine_parts(products, -1.0).astype(jnp.bfloat16))
    half_back = jnp.stack(halves, axis=1)
    products = jnp.einsum("bcij,ajk->abcik", half_back, transform, preferred_element_type=jnp.float32)
    coil_back = combine_parts(products, -1.0)
    maps = map_rows.astype(jnp.float32)
    real_part = jnp.sum(maps[:, 0] * coil_back[0] + maps[:, 1] * coil_back[1], axis=0)
    imaginary = jnp.sum(maps[:, 0] * coil_back[1] - maps[:, 1] * coil_back[0], axis=0)
    return jnp.stack([real_part, imaginary])


def tv_term(extended, first_frame, frame_total):
    widened = extended.astype(jnp.float32)
    change = widened[1:] - widened[:-1]
    position = first_frame - 1 + jnp.arange(change.shape[0], dtype=jnp.int32)
    inside = ((position >= 0) & (position <= frame_total - 2)).astype(jnp.float32)
    normed = inside[:, None, None, None] * (
        change / jnp.sqrt(jnp.sum(change * change, axis=1, keepdims=True) + SMOOTHING)
    )
    return normed[:-1] - normed[1:]


def normed_change(later, earlier, valid):
    change = later.astype(jnp.float32) - earlier.astype(jnp.float32)
    scale = jnp.sqrt(change[0] * change[0] + change[1] * change[1] + SMOOTHING)
    return valid * (change / scale)


def tv_single(images, frame_index, frame_total):
    count = lax.axis_size("frame")
    image = images[0]
    earlier = lax.ppermute(image, "frame", [(i, i + 1) for i in range(count - 1)])
    later = lax.ppermute(image, "frame", [(i + 1, i) for i in range(count - 1)])
    has_earlier = (frame_index >= 1).astype(jnp.float32)
    has_later = (frame_index <= frame_total - 2).astype(jnp.float32)
    return (normed_change(image, earlier, has_earlier) - normed_change(later, image, has_later))[None]


def body(
    images, coil_maps, kspace_data, spoke_angle, band_row, band_col, kernel_rows, kernel_cols
):
    frame_count = images.shape[0]
    extent = images.shape[-1]
    patch_side = kernel_cols.shape[-1]
    coil_count = lax.axis_size("coil")
    coil_index = lax.axis_index("coil")
    rows = extent // coil_count
    transform = transform_table(extent)
    map_rows = exchange_rows(coil_maps[0], rows, coil_count, coil_index)
    first_frame = lax.axis_index("frame") * frame_count
    frame_total = lax.axis_size("frame") * frame_count
    if frame_count == 1:
        tv_grad = tv_single(images, first_frame, frame_total)
    else:
        tv_grad = tv_term(padded(images, (("frame", 0),), 1), first_frame, frame_total)
    row_w = pick_kernels(kernel_rows, spoke_angle[0])
    col_w = pick_kernels(kernel_cols, spoke_angle[0])
    row_select = selector(band_row[0], extent, patch_side)
    col_select = selector(band_col[0], extent, patch_side)
    exact = dict(preferred_element_type=jnp.float32)
    col_placed = jnp.einsum("gjq,gkq->gjk", col_w, col_select, **exact).astype(jnp.bfloat16)
    row_placed = jnp.einsum("grj,gir->gij", row_w, row_select, **exact)
    residual = forward_residual(
        transform, images[0], coil_maps[0], kspace_data[0, 0], row_placed, col_placed
    )
    residuals = jnp.stack(
        [residual] + [rotated(residual, coil_count, shift) for shift in range(1, coil_count)]
    )
    grad_rows = backward_rows(
        transform, residuals, map_rows, row_select, row_w, col_placed, coil_index
    )
    tv_grad, grad_rows = lax.optimization_barrier((tv_grad, grad_rows.astype(jnp.bfloat16)))
    data_grad = lax.all_gather(grad_rows, "coil", axis=1, tiled=True).astype(jnp.float32)[None]
    return images.astype(jnp.float32) - STEP_SIZE * (data_grad + TV_WEIGHT * tv_grad)


def solution(mesh):
    in_specs = (
        P(("grp", "frame"), None, None, None),
        P(("grp", "coil"), None, None, None),
        P(("grp", "frame"), "coil", None, None, None),
        P(("grp", "frame"), None),
        P(("grp", "frame"), None),
        P(("grp", "frame"), None),
        P(),
        P(),
    )
    out_specs = P(("grp", "frame"), None, None, None)
    return jax.shard_map(body, mesh=mesh, in_specs=in_specs, out_specs=out_specs, check_vma=False)
```

```python
import math

import jax
import ml_dtypes
import numpy as np
import jax.numpy as jnp
from jax import lax
from jax.sharding import PartitionSpec as P


SMOOTHING = 0.05
STEP_SIZE = 1.0
TV_WEIGHT = 0.2


def padded(cells, sides, width):
    for axis, dim in sides:
        count = lax.axis_size(axis)
        ends = count - 1
        head = lax.slice_in_dim(cells, 0, width, axis=dim)
        tail = lax.slice_in_dim(cells, cells.shape[dim] - width, cells.shape[dim], axis=dim)
        cells = jnp.concatenate(
            [
                lax.ppermute(tail, axis, [(i, (i + 1) % count) for i in range(ends)]),
                cells,
                lax.ppermute(head, axis, [((i + 1) % count, i) for i in range(ends)]),
            ],
            axis=dim,
        )
    return cells


def transform_table(extent):
    indices = np.arange(extent, dtype=np.int64)
    phases = (indices[:, None] * indices[None, :] % extent).astype(np.float32)
    angle_values = np.float32(2.0 * math.pi / extent) * phases
    scaling = np.float32(1.0 / math.sqrt(extent))
    table = np.stack([np.cos(angle_values) * scaling, np.sin(angle_values) * scaling])
    return jnp.asarray(table.astype(ml_dtypes.bfloat16))


def combine_parts(products, direction):
    real_part = products[0, 0] + direction * products[1, 1]
    imaginary = products[0, 1] - direction * products[1, 0]
    return jnp.stack([real_part, imaginary])


def rotated(block, coil_count, shift):
    return lax.ppermute(block, "coil", [(i, (i + shift) % coil_count) for i in range(coil_count)])


def exchange_rows(coil_map, rows, coil_count, coil_index):
    received = [lax.dynamic_slice_in_dim(coil_map, coil_index * rows, rows, axis=1)]
    for shift in range(1, coil_count):
        target = (coil_index + shift) % coil_count
        block = lax.dynamic_slice_in_dim(coil_map, target * rows, rows, axis=1)
        received.append(rotated(block, coil_count, shift))
    return jnp.stack(received)


def selector(first_index, extent, patch_side):
    positions = jnp.arange(extent, dtype=jnp.int32)
    offsets = jnp.arange(patch_side, dtype=jnp.int32)
    wanted = first_index[:, None, None] + offsets[None, None, :]
    return (positions[None, :, None] == wanted).astype(jnp.bfloat16)


def pick_kernels(kernels, angle_ids):
    choice = (angle_ids[:, None] == jnp.arange(kernels.shape[0], dtype=jnp.int32)[None, :])
    flat = kernels.reshape(kernels.shape[0], -1)
    picked = jnp.dot(choice.astype(kernels.dtype), flat, preferred_element_type=jnp.float32)
    return picked.astype(kernels.dtype).reshape((angle_ids.shape[0],) + kernels.shape[1:])


def forward_residual(transform, frame_image, coil_map, measured, row_placed, col_placed):
    map_planes = coil_map.astype(jnp.float32)
    image_planes = frame_image.astype(jnp.float32)
    coil_image = jnp.stack(
        [
            map_planes[0] * image_planes[0] - map_planes[1] * image_planes[1],
            map_planes[0] * image_planes[1] + map_planes[1] * image_planes[0],
        ]
    ).astype(jnp.bfloat16)
    products = jnp.einsum(
        "bij,ajk->abik", coil_image, transform, preferred_element_type=jnp.float32
    )
    half_done = combine_parts(products, 1.0).astype(jnp.bfloat16)
    cos_t, sin_t = lax.optimization_barrier(transform)
    block = jnp.concatenate(
        [jnp.concatenate([cos_t, sin_t], axis=1), jnp.concatenate([-sin_t, cos_t], axis=1)]
    )
    extent = transform.shape[-1]
    kspace = jnp.dot(
        block, half_done.reshape(2 * extent, extent), preferred_element_type=jnp.float32
    ).astype(jnp.bfloat16).reshape(2, extent, extent)
    contracted = jnp.einsum("pik,gjk->pgij", kspace, col_placed, preferred_element_type=jnp.float32)
    predicted = jnp.sum(contracted * row_placed[None], axis=2)
    return predicted - measured


def backward_rows(transform, residuals, map_rows, row_select, row_w, col_placed, coil_index):
    rows = map_rows.shape[2]
    spread = (row_w.astype(jnp.float32)[None, None] * residuals[:, :, :, None, :]).astype(jnp.bfloat16)
    placed = jnp.einsum(
        "cpgrj,gjk->cpgrk", spread, col_placed, preferred_element_type=jnp.float32
    ).astype(jnp.bfloat16)
    row_table = lax.dynamic_slice_in_dim(transform, coil_index * rows, rows, axis=1)
    table_at = jnp.einsum(
        "aij,gjr->aigr", row_table, row_select, preferred_element_type=jnp.float32
    ).astype(jnp.bfloat16)
    products = jnp.einsum("aigr,cbgrk->abcik", table_at, placed, preferred_element_type=jnp.float32)
    pairs = products.reshape((4,) + products.shape[2:])
    signs = jnp.array([-1.0, 1.0], jnp.float32).reshape((2,) + (1,) * (pairs.ndim - 1))
    half_back = (pairs[:2] + signs * jnp.flip(pairs, 0)[:2]).astype(jnp.bfloat16)
    products = jnp.einsum("bcij,ajk->abcik", half_back, transform, preferred_element_type=jnp.float32)
    coil_back = combine_parts(products, -1.0)
    maps = map_rows.astype(jnp.float32)
    real_part = jnp.sum(maps[:, 0] * coil_back[0] + maps[:, 1] * coil_back[1], axis=0)
    imaginary = jnp.sum(maps[:, 0] * coil_back[1] - maps[:, 1] * coil_back[0], axis=0)
    return jnp.stack([real_part, imaginary])


def tv_term(extended, first_frame, frame_total):
    widened = extended.astype(jnp.float32)
    change = widened[1:] - widened[:-1]
    position = first_frame - 1 + jnp.arange(change.shape[0], dtype=jnp.int32)
    inside = ((position >= 0) & (position <= frame_total - 2)).astype(jnp.float32)
    normed = inside[:, None, None, None] * (
        change / jnp.sqrt(jnp.sum(change * change, axis=1, keepdims=True) + SMOOTHING)
    )
    return normed[:-1] - normed[1:]


def normed_change(later, earlier, valid):
    change = later.astype(jnp.float32) - earlier.astype(jnp.float32)
    scale = jnp.sqrt(change[0] * change[0] + change[1] * change[1] + SMOOTHING)
    return valid * (change / scale)


def tv_single(images, frame_index, frame_total):
    count = lax.axis_size("frame")
    image = images[0]
    earlier = lax.ppermute(image, "frame", [(i, i + 1) for i in range(count - 1)])
    later = lax.ppermute(image, "frame", [(i + 1, i) for i in range(count - 1)])
    has_earlier = (frame_index >= 1).astype(jnp.float32)
    has_later = (frame_index <= frame_total - 2).astype(jnp.float32)
    return (normed_change(image, earlier, has_earlier) - normed_change(later, image, has_later))[None]


def body(
    images, coil_maps, kspace_data, spoke_angle, band_row, band_col, kernel_rows, kernel_cols
):
    frame_count = images.shape[0]
    extent = images.shape[-1]
    patch_side = kernel_cols.shape[-1]
    coil_count = lax.axis_size("coil")
    coil_index = lax.axis_index("coil")
    rows = extent // coil_count
    transform = transform_table(extent)
    map_rows = exchange_rows(coil_maps[0], rows, coil_count, coil_index)
    first_frame = lax.axis_index("frame") * frame_count
    frame_total = lax.axis_size("frame") * frame_count
    if frame_count == 1:
        tv_grad = tv_single(images, first_frame, frame_total)
    else:
        tv_grad = tv_term(padded(images, (("frame", 0),), 1), first_frame, frame_total)
    row_w = pick_kernels(kernel_rows, spoke_angle[0])
    col_w = pick_kernels(kernel_cols, spoke_angle[0])
    row_select = selector(band_row[0], extent, patch_side)
    col_select = selector(band_col[0], extent, patch_side)
    exact = dict(preferred_element_type=jnp.float32)
    col_placed = jnp.einsum("gjq,gkq->gjk", col_w, col_select, **exact).astype(jnp.bfloat16)
    row_placed = jnp.einsum("grj,gir->gij", row_w, row_select, **exact)
    residual = forward_residual(
        transform, images[0], coil_maps[0], kspace_data[0, 0], row_placed, col_placed
    )
    residuals = jnp.stack(
        [residual] + [rotated(residual, coil_count, shift) for shift in range(1, coil_count)]
    )
    grad_rows = backward_rows(
        transform, residuals, map_rows, row_select, row_w, col_placed, coil_index
    )
    tv_grad, grad_rows = lax.optimization_barrier((tv_grad, grad_rows.astype(jnp.bfloat16)))
    data_grad = lax.all_gather(grad_rows, "coil", axis=1, tiled=True).astype(jnp.float32)[None]
    return images.astype(jnp.float32) - STEP_SIZE * (data_grad + TV_WEIGHT * tv_grad)


def solution(mesh):
    in_specs = (
        P(("grp", "frame"), None, None, None),
        P(("grp", "coil"), None, None, None),
        P(("grp", "frame"), "coil", None, None, None),
        P(("grp", "frame"), None),
        P(("grp", "frame"), None),
        P(("grp", "frame"), None),
        P(),
        P(),
    )
    out_specs = P(("grp", "frame"), None, None, None)
    return jax.shard_map(body, mesh=mesh, in_specs=in_specs, out_specs=out_specs, check_vma=False)
```

```python
import math

import jax
import ml_dtypes
import numpy as np
import jax.numpy as jnp
from jax import lax
from jax.sharding import PartitionSpec as P


SMOOTHING = 0.05
STEP_SIZE = 1.0
TV_WEIGHT = 0.2


def padded(cells, sides, width):
    for axis, dim in sides:
        count = lax.axis_size(axis)
        ends = count - 1
        head = lax.slice_in_dim(cells, 0, width, axis=dim)
        tail = lax.slice_in_dim(cells, cells.shape[dim] - width, cells.shape[dim], axis=dim)
        cells = jnp.concatenate(
            [
                lax.ppermute(tail, axis, [(i, (i + 1) % count) for i in range(ends)]),
                cells,
                lax.ppermute(head, axis, [((i + 1) % count, i) for i in range(ends)]),
            ],
            axis=dim,
        )
    return cells


def transform_table(extent):
    indices = np.arange(extent, dtype=np.int64)
    phases = (indices[:, None] * indices[None, :] % extent).astype(np.float32)
    angle_values = np.float32(2.0 * math.pi / extent) * phases
    scaling = np.float32(1.0 / math.sqrt(extent))
    table = np.stack([np.cos(angle_values) * scaling, np.sin(angle_values) * scaling])
    return jnp.asarray(table.astype(ml_dtypes.bfloat16))


def combine_parts(products, direction):
    real_part = products[0, 0] + direction * products[1, 1]
    imaginary = products[0, 1] - direction * products[1, 0]
    return jnp.stack([real_part, imaginary])


def rotated(block, coil_count, shift):
    return lax.ppermute(block, "coil", [(i, (i + shift) % coil_count) for i in range(coil_count)])


def exchange_rows(coil_map, rows, coil_count, coil_index):
    received = [lax.dynamic_slice_in_dim(coil_map, coil_index * rows, rows, axis=1)]
    for shift in range(1, coil_count):
        target = (coil_index + shift) % coil_count
        block = lax.dynamic_slice_in_dim(coil_map, target * rows, rows, axis=1)
        received.append(rotated(block, coil_count, shift))
    return jnp.stack(received)


def selector(first_index, extent, patch_side):
    positions = jnp.arange(extent, dtype=jnp.int32)
    offsets = jnp.arange(patch_side, dtype=jnp.int32)
    wanted = first_index[:, None, None] + offsets[None, None, :]
    return (positions[None, :, None] == wanted).astype(jnp.bfloat16)


def pick_kernels(kernels, angle_ids):
    choice = (angle_ids[:, None] == jnp.arange(kernels.shape[0], dtype=jnp.int32)[None, :])
    flat = kernels.reshape(kernels.shape[0], -1)
    picked = jnp.dot(choice.astype(kernels.dtype), flat, preferred_element_type=jnp.float32)
    return picked.astype(kernels.dtype).reshape((angle_ids.shape[0],) + kernels.shape[1:])


def forward_residual(transform, frame_image, coil_map, measured, row_placed, col_placed):
    map_planes = coil_map.astype(jnp.float32)
    image_planes = frame_image.astype(jnp.float32)
    coil_image = jnp.stack(
        [
            map_planes[0] * image_planes[0] - map_planes[1] * image_planes[1],
            map_planes[0] * image_planes[1] + map_planes[1] * image_planes[0],
        ]
    ).astype(jnp.bfloat16)
    products = jnp.einsum(
        "bij,ajk->abik", coil_image, transform, preferred_element_type=jnp.float32
    )
    half_done = combine_parts(products, 1.0).astype(jnp.bfloat16)
    cos_t, sin_t = lax.optimization_barrier(transform)
    block = jnp.concatenate(
        [jnp.concatenate([cos_t, sin_t], axis=1), jnp.concatenate([-sin_t, cos_t], axis=1)]
    )
    extent = transform.shape[-1]
    kspace = jnp.dot(
        block, half_done.reshape(2 * extent, extent), preferred_element_type=jnp.float32
    ).astype(jnp.bfloat16).reshape(2, extent, extent)
    contracted = jnp.einsum("pik,gjk->pgij", kspace, col_placed, preferred_element_type=jnp.float32)
    predicted = jnp.sum(contracted * row_placed[None], axis=2)
    return predicted - measured


def backward_rows(transform, residuals, map_rows, row_select, row_w, col_placed, coil_index):
    rows = map_rows.shape[2]
    spread = (row_w.astype(jnp.float32)[None, None] * residuals[:, :, :, None, :]).astype(jnp.bfloat16)
    placed = jnp.einsum(
        "cpgrj,gjk->cpgrk", spread, col_placed, preferred_element_type=jnp.float32
    ).astype(jnp.bfloat16)
    row_table = lax.dynamic_slice_in_dim(transform, coil_index * rows, rows, axis=1)
    table_at = jnp.einsum(
        "aij,gjr->aigr", row_table, row_select, preferred_element_type=jnp.float32
    ).astype(jnp.bfloat16)
    products = jnp.einsum("aigr,cbgrk->abcik", table_at, placed, preferred_element_type=jnp.float32)
    signs = jnp.array([[1.0, 0.0, 0.0, -1.0], [0.0, 1.0, 1.0, 0.0]], jnp.float32)
    half_back = jnp.einsum(
        "oq,qcik->ocik", signs, products.reshape((4,) + products.shape[2:]),
        precision=lax.Precision.HIGHEST,
    ).astype(jnp.bfloat16)
    products = jnp.einsum("bcij,ajk->abcik", half_back, transform, preferred_element_type=jnp.float32)
    coil_back = combine_parts(products, -1.0)
    maps = map_rows.astype(jnp.float32)
    real_part = jnp.sum(maps[:, 0] * coil_back[0] + maps[:, 1] * coil_back[1], axis=0)
    imaginary = jnp.sum(maps[:, 0] * coil_back[1] - maps[:, 1] * coil_back[0], axis=0)
    return jnp.stack([real_part, imaginary])


def tv_term(extended, first_frame, frame_total):
    widened = extended.astype(jnp.float32)
    change = widened[1:] - widened[:-1]
    position = first_frame - 1 + jnp.arange(change.shape[0], dtype=jnp.int32)
    inside = ((position >= 0) & (position <= frame_total - 2)).astype(jnp.float32)
    normed = inside[:, None, None, None] * (
        change / jnp.sqrt(jnp.sum(change * change, axis=1, keepdims=True) + SMOOTHING)
    )
    return normed[:-1] - normed[1:]


def normed_change(later, earlier, valid):
    change = later.astype(jnp.float32) - earlier.astype(jnp.float32)
    scale = jnp.sqrt(change[0] * change[0] + change[1] * change[1] + SMOOTHING)
    return valid * (change / scale)


def tv_single(images, frame_index, frame_total):
    count = lax.axis_size("frame")
    image = images[0]
    earlier = lax.ppermute(image, "frame", [(i, i + 1) for i in range(count - 1)])
    later = lax.ppermute(image, "frame", [(i + 1, i) for i in range(count - 1)])
    has_earlier = (frame_index >= 1).astype(jnp.float32)
    has_later = (frame_index <= frame_total - 2).astype(jnp.float32)
    return (normed_change(image, earlier, has_earlier) - normed_change(later, image, has_later))[None]


def body(
    images, coil_maps, kspace_data, spoke_angle, band_row, band_col, kernel_rows, kernel_cols
):
    frame_count = images.shape[0]
    extent = images.shape[-1]
    patch_side = kernel_cols.shape[-1]
    coil_count = lax.axis_size("coil")
    coil_index = lax.axis_index("coil")
    rows = extent // coil_count
    transform = transform_table(extent)
    map_rows = exchange_rows(coil_maps[0], rows, coil_count, coil_index)
    first_frame = lax.axis_index("frame") * frame_count
    frame_total = lax.axis_size("frame") * frame_count
    if frame_count == 1:
        tv_grad = tv_single(images, first_frame, frame_total)
    else:
        tv_grad = tv_term(padded(images, (("frame", 0),), 1), first_frame, frame_total)
    row_w = pick_kernels(kernel_rows, spoke_angle[0])
    col_w = pick_kernels(kernel_cols, spoke_angle[0])
    row_select = selector(band_row[0], extent, patch_side)
    col_select = selector(band_col[0], extent, patch_side)
    exact = dict(preferred_element_type=jnp.float32)
    col_placed = jnp.einsum("gjq,gkq->gjk", col_w, col_select, **exact).astype(jnp.bfloat16)
    row_placed = jnp.einsum("grj,gir->gij", row_w, row_select, **exact)
    residual = forward_residual(
        transform, images[0], coil_maps[0], kspace_data[0, 0], row_placed, col_placed
    )
    residuals = jnp.stack(
        [residual] + [rotated(residual, coil_count, shift) for shift in range(1, coil_count)]
    )
    grad_rows = backward_rows(
        transform, residuals, map_rows, row_select, row_w, col_placed, coil_index
    )
    tv_grad, grad_rows = lax.optimization_barrier((tv_grad, grad_rows.astype(jnp.bfloat16)))
    data_grad = lax.all_gather(grad_rows, "coil", axis=1, tiled=True).astype(jnp.float32)[None]
    return images.astype(jnp.float32) - STEP_SIZE * (data_grad + TV_WEIGHT * tv_grad)


def solution(mesh):
    in_specs = (
        P(("grp", "frame"), None, None, None),
        P(("grp", "coil"), None, None, None),
        P(("grp", "frame"), "coil", None, None, None),
        P(("grp", "frame"), None),
        P(("grp", "frame"), None),
        P(("grp", "frame"), None),
        P(),
        P(),
    )
    out_specs = P(("grp", "frame"), None, None, None)
    return jax.shard_map(body, mesh=mesh, in_specs=in_specs, out_specs=out_specs, check_vma=False)
```

```python
import math

import jax
import ml_dtypes
import numpy as np
import jax.numpy as jnp
from jax import lax
from jax.sharding import PartitionSpec as P


SMOOTHING = 0.05
STEP_SIZE = 1.0
TV_WEIGHT = 0.2


def padded(cells, sides, width):
    for axis, dim in sides:
        count = lax.axis_size(axis)
        ends = count - 1
        head = lax.slice_in_dim(cells, 0, width, axis=dim)
        tail = lax.slice_in_dim(cells, cells.shape[dim] - width, cells.shape[dim], axis=dim)
        cells = jnp.concatenate(
            [
                lax.ppermute(tail, axis, [(i, (i + 1) % count) for i in range(ends)]),
                cells,
                lax.ppermute(head, axis, [((i + 1) % count, i) for i in range(ends)]),
            ],
            axis=dim,
        )
    return cells


def transform_table(extent):
    indices = np.arange(extent, dtype=np.int64)
    phases = (indices[:, None] * indices[None, :] % extent).astype(np.float32)
    angle_values = np.float32(2.0 * math.pi / extent) * phases
    scaling = np.float32(1.0 / math.sqrt(extent))
    table = np.stack([np.cos(angle_values) * scaling, np.sin(angle_values) * scaling])
    return jnp.asarray(table.astype(ml_dtypes.bfloat16))


def combine_parts(products, direction):
    real_part = products[0, 0] + direction * products[1, 1]
    imaginary = products[0, 1] - direction * products[1, 0]
    return jnp.stack([real_part, imaginary])


def rotated(block, coil_count, shift):
    return lax.ppermute(block, "coil", [(i, (i + shift) % coil_count) for i in range(coil_count)])


def exchange_rows(coil_map, rows, coil_count, coil_index):
    wide = coil_map.astype(jnp.float32)
    received = [lax.dynamic_slice_in_dim(wide, coil_index * rows, rows, axis=1)]
    for shift in range(1, coil_count):
        target = (coil_index + shift) % coil_count
        block = lax.dynamic_slice_in_dim(wide, target * rows, rows, axis=1)
        received.append(rotated(block, coil_count, shift))
    return jnp.stack(received)


def selector(first_index, extent, patch_side):
    positions = jnp.arange(extent, dtype=jnp.int32)
    offsets = jnp.arange(patch_side, dtype=jnp.int32)
    wanted = first_index[:, None, None] + offsets[None, None, :]
    return (positions[None, :, None] == wanted).astype(jnp.bfloat16)


def pick_kernels(kernels, angle_ids):
    choice = (angle_ids[:, None] == jnp.arange(kernels.shape[0], dtype=jnp.int32)[None, :])
    flat = kernels.reshape(kernels.shape[0], -1)
    picked = jnp.dot(choice.astype(kernels.dtype), flat, preferred_element_type=jnp.float32)
    return picked.astype(kernels.dtype).reshape((angle_ids.shape[0],) + kernels.shape[1:])


def forward_residual(transform, frame_image, coil_map, measured, row_placed, col_placed):
    map_planes = coil_map.astype(jnp.float32)
    image_planes = frame_image.astype(jnp.float32)
    coil_image = jnp.stack(
        [
            map_planes[0] * image_planes[0] - map_planes[1] * image_planes[1],
            map_planes[0] * image_planes[1] + map_planes[1] * image_planes[0],
        ]
    ).astype(jnp.bfloat16)
    products = jnp.einsum(
        "bij,ajk->abik", coil_image, transform, preferred_element_type=jnp.float32
    )
    half_done = combine_parts(products, 1.0).astype(jnp.bfloat16)
    cos_t, sin_t = lax.optimization_barrier(transform)
    block = jnp.concatenate(
        [jnp.concatenate([cos_t, sin_t], axis=1), jnp.concatenate([-sin_t, cos_t], axis=1)]
    )
    extent = transform.shape[-1]
    kspace = jnp.dot(
        block, half_done.reshape(2 * extent, extent), preferred_element_type=jnp.float32
    ).astype(jnp.bfloat16).reshape(2, extent, extent)
    contracted = jnp.einsum("pik,gjk->pgij", kspace, col_placed, preferred_element_type=jnp.float32)
    predicted = jnp.sum(contracted * row_placed[None], axis=2)
    return predicted - measured


def backward_rows(transform, residuals, map_rows, row_select, row_w, col_placed, coil_index):
    rows = map_rows.shape[2]
    spread = (row_w.astype(jnp.float32)[None, None] * residuals[:, :, :, None, :]).astype(jnp.bfloat16)
    placed = jnp.einsum(
        "cpgrj,gjk->cpgrk", spread, col_placed, preferred_element_type=jnp.float32
    ).astype(jnp.bfloat16)
    row_table = lax.dynamic_slice_in_dim(transform, coil_index * rows, rows, axis=1)
    table_at = jnp.einsum(
        "aij,gjr->aigr", row_table, row_select, preferred_element_type=jnp.float32
    ).astype(jnp.bfloat16)
    products = jnp.einsum("aigr,cbgrk->abcik", table_at, placed, preferred_element_type=jnp.float32)
    half_back = combine_parts(products, -1.0).astype(jnp.bfloat16)
    products = jnp.einsum("bcij,ajk->abcik", half_back, transform, preferred_element_type=jnp.float32)
    coil_back = combine_parts(products, -1.0)
    maps = map_rows.astype(jnp.float32)
    real_part = jnp.sum(maps[:, 0] * coil_back[0] + maps[:, 1] * coil_back[1], axis=0)
    imaginary = jnp.sum(maps[:, 0] * coil_back[1] - maps[:, 1] * coil_back[0], axis=0)
    return jnp.stack([real_part, imaginary])


def tv_term(extended, first_frame, frame_total):
    widened = extended.astype(jnp.float32)
    change = widened[1:] - widened[:-1]
    position = first_frame - 1 + jnp.arange(change.shape[0], dtype=jnp.int32)
    inside = ((position >= 0) & (position <= frame_total - 2)).astype(jnp.float32)
    normed = inside[:, None, None, None] * (
        change / jnp.sqrt(jnp.sum(change * change, axis=1, keepdims=True) + SMOOTHING)
    )
    return normed[:-1] - normed[1:]


def normed_change(later, earlier, valid):
    change = later.astype(jnp.float32) - earlier.astype(jnp.float32)
    scale = jnp.sqrt(change[0] * change[0] + change[1] * change[1] + SMOOTHING)
    return valid * (change / scale)


def tv_single(images, frame_index, frame_total):
    count = lax.axis_size("frame")
    image = images[0]
    earlier = lax.ppermute(image, "frame", [(i, i + 1) for i in range(count - 1)])
    later = lax.ppermute(image, "frame", [(i + 1, i) for i in range(count - 1)])
    has_earlier = (frame_index >= 1).astype(jnp.float32)
    has_later = (frame_index <= frame_total - 2).astype(jnp.float32)
    return (normed_change(image, earlier, has_earlier) - normed_change(later, image, has_later))[None]


def body(
    images, coil_maps, kspace_data, spoke_angle, band_row, band_col, kernel_rows, kernel_cols
):
    frame_count = images.shape[0]
    extent = images.shape[-1]
    patch_side = kernel_cols.shape[-1]
    coil_count = lax.axis_size("coil")
    coil_index = lax.axis_index("coil")
    rows = extent // coil_count
    transform = transform_table(extent)
    map_rows = exchange_rows(coil_maps[0], rows, coil_count, coil_index)
    first_frame = lax.axis_index("frame") * frame_count
    frame_total = lax.axis_size("frame") * frame_count
    if frame_count == 1:
        tv_grad = tv_single(images, first_frame, frame_total)
    else:
        tv_grad = tv_term(padded(images, (("frame", 0),), 1), first_frame, frame_total)
    row_w = pick_kernels(kernel_rows, spoke_angle[0])
    col_w = pick_kernels(kernel_cols, spoke_angle[0])
    row_select = selector(band_row[0], extent, patch_side)
    col_select = selector(band_col[0], extent, patch_side)
    exact = dict(preferred_element_type=jnp.float32)
    col_placed = jnp.einsum("gjq,gkq->gjk", col_w, col_select, **exact).astype(jnp.bfloat16)
    row_placed = jnp.einsum("grj,gir->gij", row_w, row_select, **exact)
    residual = forward_residual(
        transform, images[0], coil_maps[0], kspace_data[0, 0], row_placed, col_placed
    )
    residuals = jnp.stack(
        [residual] + [rotated(residual, coil_count, shift) for shift in range(1, coil_count)]
    )
    grad_rows = backward_rows(
        transform, residuals, map_rows, row_select, row_w, col_placed, coil_index
    )
    tv_grad, grad_rows = lax.optimization_barrier((tv_grad, grad_rows.astype(jnp.bfloat16)))
    data_grad = lax.all_gather(grad_rows, "coil", axis=1, tiled=True).astype(jnp.float32)[None]
    return images.astype(jnp.float32) - STEP_SIZE * (data_grad + TV_WEIGHT * tv_grad)


def solution(mesh):
    in_specs = (
        P(("grp", "frame"), None, None, None),
        P(("grp", "coil"), None, None, None),
        P(("grp", "frame"), "coil", None, None, None),
        P(("grp", "frame"), None),
        P(("grp", "frame"), None),
        P(("grp", "frame"), None),
        P(),
        P(),
    )
    out_specs = P(("grp", "frame"), None, None, None)
    return jax.shard_map(body, mesh=mesh, in_specs=in_specs, out_specs=out_specs, check_vma=False)
```
